32 devices in a mesh: groups: 2 (over y), dp: 8 (over z, core), vocab: 2 (over x).
Axes of the slice: x: 2, y: 2, z: 4, core: 2. Of those that a mesh axis runs over, the one named last changes fastest.
Arguments:
- teacher_hidden: bfloat16 [128, 5120], P(('groups', 'dp')), parts along dimension 0, may hold values from -110 to 110
- teacher_head: bfloat16 [5120, 98304], P(None, ('dp', 'vocab')), may hold values from -0.078125 to 0.078125
- map_dest: int32 [768, 4], P(('dp', 'vocab')), may hold values from 0 to 7, all different within a row; in each aligned block of 48 rows (0 to 47, 48 to 95, ...) at most 24 rows name the same one
- map_slot: int32 [768, 4], P(('dp', 'vocab')), may hold values from 0 to 31
- map_weight: bfloat16 [768, 4, 128, 128], P(('dp', 'vocab')), may hold values from 0.019897461 to 1
- student_hidden: bfloat16 [128, 4096], P(('groups', 'dp')), parts along dimension 0, may hold values from -110 to 110
- student_head: bfloat16 [4096, 65536], P(None, ('dp', 'vocab')), may hold values from -0.09375 to 0.09375
- targets: int32 [128], P(('groups', 'dp')), parts along dimension 0, may hold values from 0 to 65535
Outputs:
- grad_hidden: bfloat16 [128, 4096], P(('groups', 'dp', 'vocab')), parts along dimension 0
The draws below stay inside these ranges and needn't reach their ends.
There are 2 independent parts, one for each index of `groups`. The reference program is written for one: setup_inputs(seed, part) draws one part's arguments, and reference() takes and returns one part's arrays. A program takes and returns all parts, laid end to end along the dimension named above; an argument that names none is the same for every part. Nothing has to cross between parts.
Inputs may be any that keep to these rules, and one draw needn't show every extreme that they name: `map_dest`: the 4 entries of a row differ. Among the 48 rows of one device (aligned blocks of rows) no value appears more than 24 times, and some value appears exactly 24 times.
All inputs are finite; a program needn't handle non-finite values.
Results may differ from the reference program's by a relative error of at most 0.012.
Values may be sent and summed in bfloat16 or wider, within the bound.
No kernel may reach another device: no remote copies, remote signals or barrier semaphores. Data moves between devices by JAX's collectives and lax.ppermute only.
A program may use at most 192 MiB of HBM per device.

```python
import math
import jax
import jax.numpy as jnp
import numpy as np
from jax import lax

DT = 5120
DS = 4096
VT = 98304
VS = 65536
BLOCK = 128
R = 4
TOKENS = 64
NTB = 768
TBLK_DEV = 48
SBLK_DEV = 32
CAP = 24
N_DP = 8
N_VOCAB = 2


def hidden_draw(key, rows, width):
    base_key, scale_key = jax.random.split(key, 2)
    scales = jnp.exp(jax.random.uniform(scale_key, (rows, 1), jnp.float32, math.log(2.0), math.log(16.0)))
    values = jnp.clip(jax.random.normal(base_key, (rows, width), jnp.float32), -6.0, 6.0)
    return (values * scales).astype(jnp.bfloat16)


def draw_teacher_hidden(key, part):
    return hidden_draw(jax.random.fold_in(key, 11), TOKENS, DT)


def draw_student_hidden(key, part):
    return hidden_draw(jax.random.fold_in(key, 23), TOKENS, DS)


def plant(values, key, low, high):
    longest = values.shape.index(max(values.shape))
    spots = []
    for shift in (0, 1):
        where = [jax.random.randint(jax.random.fold_in(key, axis), (), 0, length) for axis, length in enumerate(values.shape)]
        where[longest] = (where[longest] + shift) % values.shape[longest]
        spots.append(tuple(where))
    return values.at[spots[0]].set(low).at[spots[1]].set(high)


def block_levels(stream_key, extent, cuts, smallest, largest):
    def one(dim, parts):
        heights = jax.random.uniform(jax.random.fold_in(jax.random.fold_in(stream_key, 6), dim), (parts,), jnp.float32, smallest / len(cuts), largest / len(cuts))
        return jnp.repeat(jnp.exp(heights), extent[dim] // parts).reshape((-1,) + (1,) * (len(extent) - dim - 1))

    gain = one(*cuts[0])
    for cut in cuts[1:]:
        gain = gain * one(*cut)
    return gain


def cumulative_ranks(count, skew):
    loads = [(1 << 20) // math.isqrt(standing ** skew) + 1 for standing in range(1, count + 1)]
    spread = 1 + sum(loads) // (1 << 30)
    return np.cumsum(np.array([max(1, weight // spread) for weight in loads]))


def skewed_ids(stream_key, dims, number_of, slope):
    grid = cumulative_ranks(number_of, slope)
    lot = jax.random.randint(jax.random.fold_in(stream_key, 1), dims, 0, int(grid[number_of - 1]))
    standing = jnp.searchsorted(jnp.asarray(grid, jnp.int32), lot, side="right")
    return jax.random.permutation(jax.random.fold_in(stream_key, 2), number_of)[standing].astype(jnp.int32)


def assign_block(stream_key, own, number, rows, count, top, bound, skew):
    order = jax.random.permutation(stream_key, count)
    packed, ordinary = load_shares(count, rows * top, bound, skew, True), load_shares(count, rows * top, bound, skew, False)
    places = jnp.arange(count)

    def named(tallies, rotation):
        used = int((tallies > 0).sum())
        fixed = max(1, used // 4)
        moved = fixed + (places - fixed + rotation * (used - fixed)) % max(1, count - fixed)
        return jnp.zeros((count,), jnp.int32).at[order[jnp.where(places < fixed, places, moved)]].set(jnp.asarray(tallies, jnp.int32))

    tallies = jnp.where(number % 4 == 0, named(packed, number // 4), named(ordinary, number - number // 4 - 1))
    mixed = jax.random.permutation(jax.random.fold_in(own, 3), count)
    donor, sink = mixed[0:count // 2 * 2:2], mixed[1:count // 2 * 2:2]
    margin = jnp.minimum(tallies[donor] - 1, bound - tallies[sink]) // 2
    margin = jnp.where((donor == order[0]) | (sink == order[0]) | (tallies[sink] == 0), 0, jnp.maximum(margin, 0))
    moved = jax.random.randint(jax.random.fold_in(own, 4), (count // 2,), 0, 1 << 20) % (margin + 1)
    tallies = tallies.at[donor].add(-moved).at[sink].add(moved)
    members = jnp.searchsorted(jnp.cumsum(tallies), jnp.arange(rows * top), side="right").astype(jnp.int32)
    listing = members.reshape(top, rows).T
    listing = listing[jax.random.permutation(jax.random.fold_in(own, 1), rows)]
    rotation = jax.random.randint(jax.random.fold_in(own, 2), (rows, 1), 0, top)
    return jnp.take_along_axis(listing, (jnp.arange(top)[None, :] + rotation) % top, axis=1)


def load_shares(amount, total, reach, skew, full):
    portions = [(1 << 20) // math.isqrt(grade ** skew) + 1 for grade in range(1, amount + 1)]
    largest = reach if full else min(reach, max(-(-total // amount), total * portions[0] // sum(portions)))
    least = 1 if total - largest >= amount - 1 else 0
    given, rest = [largest] + [least] * (amount - 1), total - largest - least * (amount - 1)
    while rest > 0:
        candidates = [i for i in range(1, amount) if given[i] < largest] or [i for i in range(1, amount) if given[i] < reach]
        mass, budget = sum([portions[i] for i in candidates]), rest
        for i in candidates:
            extra = min(reach - given[i], max(1, budget * portions[i] // mass), rest)
            given[i] = given[i] + extra
            rest = rest - extra
    return np.array(given)


def centred(own_key, dims, scale, most, shards=(), kind=jnp.bfloat16):
    result = jax.random.normal(own_key, dims, jnp.float32) * scale
    if len(shards) > 0:
        result = block_levels(own_key, dims, shards, -0.22, 0.18) * result
    return jnp.clip(result, min=-most, max=most).astype(kind)


def setup_inputs(seed: int = 0, part: int = 0) -> dict:
    keys = jax.random.split(jax.random.key(seed), 9)
    part_splits = jax.random.split(jax.random.fold_in(keys[8], part), 9)
    teacher_hidden = draw_teacher_hidden(jax.random.fold_in(jax.random.fold_in(keys[8], part), 71), part)
    teacher_head = centred(keys[1], (DT, VT), DT ** -0.5, 0.078125, ((1, 16),))
    map_dest_keys = jax.random.split(jax.random.fold_in(keys[2], 1), NTB // TBLK_DEV)
    map_dest_turns = jax.random.permutation(jax.random.fold_in(keys[2], 3), NTB // TBLK_DEV)
    map_dest = jax.vmap(lambda own, number: assign_block(jax.random.fold_in(keys[2], 2), own, number, TBLK_DEV, N_DP, R, CAP, 2))(map_dest_keys, map_dest_turns).reshape((NTB, R))
    map_slot = plant(jax.random.randint(keys[3], (NTB, R), 0, SBLK_DEV), jax.random.fold_in(keys[3], 1), 0, SBLK_DEV - 1).astype(jnp.int32)
    map_weight = jnp.clip(jnp.exp(math.log(1.0) - 3.9171631 * jax.random.uniform(keys[4], (NTB, R, BLOCK, BLOCK), jnp.float32) ** block_levels(keys[4], (NTB, R, BLOCK, BLOCK), ((0, 16),), -0.2, 0.2)), 0.019897461, 1.0).astype(jnp.bfloat16)
    student_hidden = draw_student_hidden(jax.random.fold_in(jax.random.fold_in(keys[8], part), 71), part)
    student_head = centred(keys[6], (DS, VS), DS ** -0.5, 0.09375, ((1, 16),))
    targets = plant(skewed_ids(part_splits[7], (TOKENS,), VS, 2), jax.random.fold_in(part_splits[7], 3), 0, VS - 1).astype(jnp.int32)
    return {"teacher_hidden": teacher_hidden, "teacher_head": teacher_head, "map_dest": map_dest, "map_slot": map_slot, "map_weight": map_weight, "student_hidden": student_hidden, "student_head": student_head, "targets": targets}


hard_weight = 0.25
loss_scale = 64.0


def reference(teacher_hidden, teacher_head, map_dest, map_slot, map_weight, student_hidden, student_head, targets):
    teacher_logits = jnp.dot(teacher_hidden, teacher_head, preferred_element_type=jnp.float32)
    teacher_peak = jnp.max(teacher_logits, axis=1, keepdims=True)
    teacher_weights = jnp.exp(teacher_logits - teacher_peak).astype(jnp.bfloat16)
    prob_blocks = jnp.transpose(teacher_weights.reshape(TOKENS, VT // BLOCK, BLOCK), (1, 0, 2))
    teacher_coord = (jnp.arange(VT // BLOCK, dtype=jnp.int32) // TBLK_DEV) % N_VOCAB
    dest_block = ((map_dest * N_VOCAB + teacher_coord[:, None]) * SBLK_DEV + map_slot).astype(jnp.int32)

    def accumulate(mapped, scan_item):
        prob_block, weight_block, block_ids = scan_item
        mapped_terms = jnp.einsum("tc,rcd->rtd", prob_block.astype(jnp.float32), weight_block.astype(jnp.float32))
        rounded = lax.optimization_barrier(mapped_terms.astype(jnp.bfloat16))
        return mapped.at[block_ids].add(rounded.astype(jnp.float32)), None

    start_mapped = jnp.zeros((VS // BLOCK, TOKENS, BLOCK), jnp.float32)
    mapped, unused_out = lax.scan(accumulate, start_mapped, (prob_blocks, map_weight, dest_block))
    mapped = jnp.transpose(mapped, (1, 0, 2)).reshape(TOKENS, VS)
    target_total = jnp.sum(mapped, axis=1, keepdims=True)
    target_probs = mapped / target_total
    student_logits = jnp.dot(student_hidden, student_head, preferred_element_type=jnp.float32)
    student_peak = jnp.max(student_logits, axis=1, keepdims=True)
    student_exp = jnp.exp(student_logits - student_peak)
    student_probs = student_exp / jnp.sum(student_exp, axis=1, keepdims=True)
    target_hits = (jnp.arange(VS, dtype=jnp.int32)[None, :] == targets[:, None]).astype(jnp.float32)
    logit_grad = (loss_scale * (student_probs - (1.0 - hard_weight) * target_probs - hard_weight * target_hits)).astype(jnp.bfloat16)
    gradient = jnp.dot(logit_grad, student_head.T, preferred_element_type=jnp.float32)
    return gradient.astype(jnp.bfloat16)
```

```python
import jax
import jax.numpy as jnp
from jax import lax
from jax.sharding import PartitionSpec as P

hard_weight = 0.25
loss_scale = 64.0


def _code(values):
    return values.astype(jnp.float32).astype(jnp.bfloat16)


def _decode(values):
    return jnp.round(values.astype(jnp.float32)).astype(jnp.int32)


def on_device(
    teacher_hidden,
    teacher_head,
    map_dest,
    map_slot,
    map_weight,
    student_hidden,
    student_head,
    targets,
):
    dp_count = lax.axis_size("dp")
    vocab_count = lax.axis_size("vocab")
    my_dp = lax.axis_index("dp")
    my_vocab = lax.axis_index("vocab")
    block_size = map_weight.shape[2]
    teacher_blocks = map_dest.shape[0]
    fan_count = map_dest.shape[1]
    student_cols = student_head.shape[1]
    student_blocks = student_cols // block_size
    capacity = max(2, (teacher_blocks * fan_count + dp_count - 1) // dp_count)
    device_flat = my_dp * vocab_count + my_vocab
    item_count = teacher_blocks * fan_count
    local_tokens = teacher_hidden.shape[0]
    teacher_width = teacher_hidden.shape[1]
    student_width = student_hidden.shape[1]

    coded = jnp.concatenate(
        [
            _code(map_dest.reshape(item_count)),
            _code(map_slot.reshape(item_count)),
            _code(targets // 256),
            _code(targets % 256),
        ]
    )
    extra_width = -(-coded.shape[0] // local_tokens)
    extra_width = -(-extra_width // 128) * 128
    coded = jnp.pad(coded, (0, extra_width * local_tokens - coded.shape[0]))
    packed = jnp.concatenate(
        [teacher_hidden, student_hidden, coded.reshape(local_tokens, extra_width)], axis=1
    )
    gathered = lax.all_gather(packed, "dp", axis=0, tiled=True)
    tokens_all = gathered.shape[0]
    teacher_all = gathered[:, :teacher_width]
    student_all = gathered[:, teacher_width : teacher_width + student_width]
    extra_all = gathered[:, teacher_width + student_width :].reshape(
        dp_count, local_tokens * extra_width
    )
    src_dest = _decode(extra_all[:, :item_count])
    src_slot = _decode(extra_all[:, item_count : 2 * item_count])
    t_hi = _decode(extra_all[:, 2 * item_count : 2 * item_count + local_tokens])
    t_lo = _decode(extra_all[:, 2 * item_count + local_tokens : 2 * item_count + 2 * local_tokens])
    all_targets = (t_hi * 256 + t_lo).reshape(tokens_all)

    teacher_logits = jnp.dot(teacher_all, teacher_head, preferred_element_type=jnp.float32)
    teacher_local_peak = jnp.max(teacher_logits, axis=1)
    teacher_weights = jnp.exp(teacher_logits - teacher_local_peak[:, None]).astype(jnp.bfloat16)
    prob_blocks = teacher_weights.reshape(tokens_all, teacher_blocks, block_size)
    mapped_terms = jnp.einsum(
        "gkc,krcd->krgd", prob_blocks, map_weight, preferred_element_type=jnp.float32
    ).astype(jnp.bfloat16)
    mapped_mass = jnp.sum(mapped_terms.astype(jnp.float32), axis=(0, 1, 3))

    dest_flat = map_dest.reshape(item_count)
    dest_onehot = (dest_flat[:, None] == jnp.arange(dp_count, dtype=jnp.int32)[None, :]).astype(
        jnp.int32
    )
    earlier_same = jnp.sum(jnp.cumsum(dest_onehot, axis=0) * dest_onehot, axis=1) - 1
    slot_index = dest_flat * capacity + earlier_same
    placement = (
        jnp.arange(dp_count * capacity, dtype=jnp.int32)[:, None] == slot_index[None, :]
    ).astype(jnp.bfloat16)
    outgoing = jnp.dot(
        placement,
        mapped_terms.reshape(item_count, tokens_all * block_size),
        preferred_element_type=jnp.float32,
    )
    outgoing = outgoing.astype(jnp.bfloat16).reshape(dp_count, capacity, tokens_all, block_size)
    incoming = lax.all_to_all(outgoing, "dp", split_axis=0, concat_axis=0, tiled=True)

    student_logits = jnp.dot(student_all, student_head, preferred_element_type=jnp.float32)
    student_local_peak = jnp.max(student_logits, axis=1)
    student_local_total = jnp.sum(jnp.exp(student_logits - student_local_peak[:, None]), axis=1)

    stats = jnp.stack(
        [teacher_local_peak, mapped_mass, student_local_peak, student_local_total]
    )
    all_stats = lax.all_gather(stats, ("dp", "vocab"), axis=0, tiled=False)
    teacher_peak = jnp.max(all_stats[:, 0], axis=0)
    teacher_scale = jnp.exp(all_stats[:, 0] - teacher_peak[None, :])
    target_total = jnp.sum(teacher_scale * all_stats[:, 1], axis=0)
    student_peak = jnp.max(all_stats[:, 2], axis=0)
    student_total = jnp.sum(
        jnp.exp(all_stats[:, 2] - student_peak[None, :]) * all_stats[:, 3], axis=0
    )
    source_scale = teacher_scale.reshape(dp_count, vocab_count, tokens_all)[:, my_vocab]

    is_mine = (src_dest == my_dp).astype(jnp.int32)
    rank = jnp.cumsum(is_mine, axis=1) - 1
    at_cap = (
        (rank[:, :, None] == jnp.arange(capacity, dtype=jnp.int32)[None, None, :])
        & (is_mine[:, :, None] > 0)
    ).astype(jnp.float32)
    at_slot = (
        src_slot[:, :, None] == jnp.arange(student_blocks, dtype=jnp.int32)[None, None, :]
    ).astype(jnp.float32)
    marks = jnp.einsum("xec,xes->xcs", at_cap, at_slot)
    scaled_in = incoming.astype(jnp.float32) * source_scale[:, None, :, None]
    mapped = jnp.einsum(
        "xcs,xctd->tsd", marks, scaled_in, precision=lax.Precision.HIGHEST,
        preferred_element_type=jnp.float32,
    ).reshape(tokens_all, student_cols)

    target_probs = mapped / target_total[:, None]
    student_probs = jnp.exp(student_logits - student_peak[:, None]) / student_total[:, None]
    columns = device_flat * student_cols + jnp.arange(student_cols, dtype=jnp.int32)
    target_hits = (all_targets[:, None] == columns[None, :]).astype(jnp.float32)
    logit_grad = (
        loss_scale
        * (student_probs - (1.0 - hard_weight) * target_probs - hard_weight * target_hits)
    ).astype(jnp.bfloat16)
    gradient = lax.psum_scatter(
        lax.dot_general(
            logit_grad, student_head, (((1,), (1,)), ((), ())), preferred_element_type=jnp.float32
        ),
        ("dp", "vocab"),
        scatter_dimension=0,
        tiled=True,
    )
    return gradient.astype(jnp.bfloat16)


def solution(mesh):
    placed = (
        P(("groups", "dp"), None),
        P(None, ("dp", "vocab")),
        P(("dp", "vocab"), None),
        P(("dp", "vocab"), None),
        P(("dp", "vocab"), None, None, None),
        P(("groups", "dp"), None),
        P(None, ("dp", "vocab")),
        P(("groups", "dp")),
    )
    return jax.shard_map(
        on_device,
        mesh=mesh,
        in_specs=placed,
        out_specs=P(("groups", "dp", "vocab"), None),
        check_vma=False,
    )
```

```python
import jax
import jax.numpy as jnp
from jax import lax
from jax.sharding import PartitionSpec as P

hard_weight = 0.25
loss_scale = 64.0


def _code(values):
    return values.astype(jnp.float32).astype(jnp.bfloat16)


def _decode(values):
    return jnp.round(values.astype(jnp.float32)).astype(jnp.int32)


def on_device(
    teacher_hidden,
    teacher_head,
    map_dest,
    map_slot,
    map_weight,
    student_hidden,
    student_head,
    targets,
):
    dp_count = lax.axis_size("dp")
    vocab_count = lax.axis_size("vocab")
    my_dp = lax.axis_index("dp")
    my_vocab = lax.axis_index("vocab")
    block_size = map_weight.shape[2]
    teacher_blocks = map_dest.shape[0]
    fan_count = map_dest.shape[1]
    student_cols = student_head.shape[1]
    student_blocks = student_cols // block_size
    capacity = max(2, (teacher_blocks * fan_count + dp_count - 1) // dp_count)
    device_flat = my_dp * vocab_count + my_vocab
    item_count = teacher_blocks * fan_count
    local_tokens = teacher_hidden.shape[0]
    teacher_width = teacher_hidden.shape[1]
    student_width = student_hidden.shape[1]

    coded = jnp.concatenate(
        [
            _code(map_dest.reshape(item_count)),
            _code(map_slot.reshape(item_count)),
            _code(targets // 256),
            _code(targets % 256),
        ]
    )
    extra_width = -(-coded.shape[0] // local_tokens)
    extra_width = -(-extra_width // 128) * 128
    coded = jnp.pad(coded, (0, extra_width * local_tokens - coded.shape[0]))
    packed = jnp.concatenate(
        [teacher_hidden, student_hidden, coded.reshape(local_tokens, extra_width)], axis=1
    )
    gathered = lax.all_gather(packed, "dp", axis=0, tiled=True)
    tokens_all = gathered.shape[0]
    teacher_all = gathered[:, :teacher_width]
    student_all = gathered[:, teacher_width : teacher_width + student_width]
    extra_all = gathered[:, teacher_width + student_width :].reshape(
        dp_count, local_tokens * extra_width
    )
    src_dest = _decode(extra_all[:, :item_count])
    src_slot = _decode(extra_all[:, item_count : 2 * item_count])
    t_hi = _decode(extra_all[:, 2 * item_count : 2 * item_count + local_tokens])
    t_lo = _decode(extra_all[:, 2 * item_count + local_tokens : 2 * item_count + 2 * local_tokens])
    all_targets = (t_hi * 256 + t_lo).reshape(tokens_all)

    teacher_logits = jnp.dot(teacher_all, teacher_head, preferred_element_type=jnp.float32)
    teacher_local_peak = jnp.max(teacher_logits, axis=1)
    teacher_weights = jnp.exp(teacher_logits - teacher_local_peak[:, None]).astype(jnp.bfloat16)
    prob_blocks = teacher_weights.reshape(tokens_all, teacher_blocks, block_size)
    mapped_terms = jnp.einsum(
        "gkc,krcd->krgd", prob_blocks, map_weight, preferred_element_type=jnp.float32
    ).astype(jnp.bfloat16)
    mapped_mass = jnp.sum(mapped_terms.astype(jnp.float32), axis=(0, 1, 3))

    dest_flat = map_dest.reshape(item_count)
    dest_onehot = (dest_flat[:, None] == jnp.arange(dp_count, dtype=jnp.int32)[None, :]).astype(
        jnp.int32
    )
    earlier_same = jnp.sum(jnp.cumsum(dest_onehot, axis=0) * dest_onehot, axis=1) - 1
    slot_index = dest_flat * capacity + earlier_same
    placement = (
        jnp.arange(dp_count * capacity, dtype=jnp.int32)[:, None] == slot_index[None, :]
    ).astype(jnp.bfloat16)
    outgoing = jnp.dot(
        placement,
        mapped_terms.reshape(item_count, tokens_all * block_size),
        preferred_element_type=jnp.float32,
    )
    outgoing = outgoing.astype(jnp.bfloat16).reshape(dp_count, capacity, tokens_all, block_size)
    incoming = lax.all_to_all(outgoing, "dp", split_axis=0, concat_axis=0, tiled=True)

    student_logits = jnp.dot(student_all, student_head, preferred_element_type=jnp.float32)
    student_local_peak = jnp.max(student_logits, axis=1)
    student_local_total = jnp.sum(jnp.exp(student_logits - student_local_peak[:, None]), axis=1)

    stats = jnp.stack(
        [teacher_local_peak, mapped_mass, student_local_peak, student_local_total]
    )
    all_stats = lax.all_gather(stats, ("dp", "vocab"), axis=0, tiled=False)
    teacher_peak = jnp.max(all_stats[:, 0], axis=0)
    teacher_scale = jnp.exp(all_stats[:, 0] - teacher_peak[None, :])
    target_total = jnp.sum(teacher_scale * all_stats[:, 1], axis=0)
    student_peak = jnp.max(all_stats[:, 2], axis=0)
    student_total = jnp.sum(
        jnp.exp(all_stats[:, 2] - student_peak[None, :]) * all_stats[:, 3], axis=0
    )
    source_scale = teacher_scale.reshape(dp_count, vocab_count, tokens_all)[:, my_vocab]

    is_mine = (src_dest == my_dp).astype(jnp.int32)
    rank = jnp.cumsum(is_mine, axis=1) - 1
    at_cap = (
        (rank[:, :, None] == jnp.arange(capacity, dtype=jnp.int32)[None, None, :])
        & (is_mine[:, :, None] > 0)
    ).astype(jnp.float32)
    at_slot = (
        src_slot[:, :, None] == jnp.arange(student_blocks, dtype=jnp.int32)[None, None, :]
    ).astype(jnp.float32)
    marks = jnp.einsum("xec,xes->xcs", at_cap, at_slot)
    scaled_in = incoming.astype(jnp.float32) * source_scale[:, None, :, None]
    mapped = jnp.einsum(
        "xcs,xctd->tsd", marks, scaled_in, precision=lax.Precision.HIGHEST,
        preferred_element_type=jnp.float32,
    ).reshape(tokens_all, student_cols)

    target_probs = mapped / target_total[:, None]
    student_probs = jnp.exp(student_logits - student_peak[:, None]) / student_total[:, None]
    columns = device_flat * student_cols + jnp.arange(student_cols, dtype=jnp.int32)
    target_hits = (all_targets[:, None] == columns[None, :]).astype(jnp.float32)
    logit_grad = (
        loss_scale
        * (student_probs - (1.0 - hard_weight) * target_probs - hard_weight * target_hits)
    ).astype(jnp.bfloat16)
    partial = lax.dot_general(
        logit_grad, student_head, (((1,), (1,)), ((), ())), preferred_element_type=jnp.float32
    ).astype(jnp.bfloat16)
    shard_count = dp_count * vocab_count
    partial = partial.reshape(shard_count, tokens_all // shard_count, partial.shape[1])
    received = lax.all_to_all(partial, ("dp", "vocab"), split_axis=0, concat_axis=0, tiled=True)
    gradient = jnp.sum(received.astype(jnp.float32), axis=0)
    return gradient.astype(jnp.bfloat16)


def solution(mesh):
    placed = (
        P(("groups", "dp"), None),
        P(None, ("dp", "vocab")),
        P(("dp", "vocab"), None),
        P(("dp", "vocab"), None),
        P(("dp", "vocab"), None, None, None),
        P(("groups", "dp"), None),
        P(None, ("dp", "vocab")),
        P(("groups", "dp")),
    )
    return jax.shard_map(
        on_device,
        mesh=mesh,
        in_specs=placed,
        out_specs=P(("groups", "dp", "vocab"), None),
        check_vma=False,
    )
```

```python
import jax
import jax.numpy as jnp
from jax import lax
from jax.sharding import PartitionSpec as P

hard_weight = 0.25
loss_scale = 64.0


def _code(values):
    return values.astype(jnp.float32).astype(jnp.bfloat16)


def _decode(values):
    return jnp.round(values.astype(jnp.float32)).astype(jnp.int32)


def on_device(
    teacher_hidden,
    teacher_head,
    map_dest,
    map_slot,
    map_weight,
    student_hidden,
    student_head,
    targets,
):
    dp_count = lax.axis_size("dp")
    vocab_count = lax.axis_size("vocab")
    my_dp = lax.axis_index("dp")
    my_vocab = lax.axis_index("vocab")
    block_size = map_weight.shape[2]
    teacher_blocks = map_dest.shape[0]
    fan_count = map_dest.shape[1]
    student_cols = student_head.shape[1]
    student_blocks = student_cols // block_size
    device_flat = my_dp * vocab_count + my_vocab
    item_count = teacher_blocks * fan_count
    local_tokens = teacher_hidden.shape[0]
    teacher_width = teacher_hidden.shape[1]
    student_width = student_hidden.shape[1]

    coded = jnp.concatenate([_code(targets // 256), _code(targets % 256)])
    extra_width = -(-coded.shape[0] // local_tokens)
    extra_width = -(-extra_width // 128) * 128
    coded = jnp.pad(coded, (0, extra_width * local_tokens - coded.shape[0]))
    packed = jnp.concatenate(
        [teacher_hidden, student_hidden, coded.reshape(local_tokens, extra_width)], axis=1
    )
    gathered = lax.all_gather(packed, "dp", axis=0, tiled=True)
    tokens_all = gathered.shape[0]
    teacher_all = gathered[:, :teacher_width]
    student_all = gathered[:, teacher_width : teacher_width + student_width]
    extra_all = gathered[:, teacher_width + student_width :].reshape(
        dp_count, local_tokens * extra_width
    )
    t_hi = _decode(extra_all[:, :local_tokens])
    t_lo = _decode(extra_all[:, local_tokens : 2 * local_tokens])
    all_targets = (t_hi * 256 + t_lo).reshape(tokens_all)

    teacher_logits = jnp.dot(teacher_all, teacher_head, preferred_element_type=jnp.float32)
    teacher_local_peak = jnp.max(teacher_logits, axis=1)
    teacher_weights = jnp.exp(teacher_logits - teacher_local_peak[:, None]).astype(jnp.bfloat16)
    prob_blocks = teacher_weights.reshape(tokens_all, teacher_blocks, block_size)
    mapped_terms = jnp.einsum(
        "gkc,krcd->krgd", prob_blocks, map_weight, preferred_element_type=jnp.float32
    ).astype(jnp.bfloat16)
    mapped_mass = jnp.sum(mapped_terms.astype(jnp.float32), axis=(0, 1, 3))

    relative = jnp.bitwise_xor(map_dest.reshape(item_count), my_dp)
    row = relative * student_blocks + map_slot.reshape(item_count)
    placement = (
        jnp.arange(dp_count * student_blocks, dtype=jnp.int32)[:, None] == row[None, :]
    ).astype(jnp.bfloat16)
    held = jnp.dot(
        placement,
        mapped_terms.reshape(item_count, tokens_all * block_size),
        preferred_element_type=jnp.float32,
    ).reshape(dp_count, student_blocks, tokens_all, block_size)

    student_logits = jnp.dot(student_all, student_head, preferred_element_type=jnp.float32)
    student_local_peak = jnp.max(student_logits, axis=1)
    student_local_total = jnp.sum(jnp.exp(student_logits - student_local_peak[:, None]), axis=1)

    peak, mass = teacher_local_peak, mapped_mass
    s_peak, s_total = student_local_peak, student_local_total

    def merge(stats, other):
        new_peak = jnp.maximum(stats[0], other[0])
        new_s_peak = jnp.maximum(stats[2], other[2])
        own, far = jnp.exp(stats[0] - new_peak), jnp.exp(other[0] - new_peak)
        s_own, s_far = jnp.exp(stats[2] - new_s_peak), jnp.exp(other[2] - new_s_peak)
        merged = jnp.stack(
            [new_peak, stats[1] * own + other[1] * far, new_s_peak,
             stats[3] * s_own + other[3] * s_far]
        )
        return merged, own, far

    stats = jnp.stack([peak, mass, s_peak, s_total])
    stage = 1
    while stage < dp_count:
        pairs = [(j, j ^ stage) for j in range(dp_count)]
        halves = held.reshape(held.shape[0] // 2, 2, student_blocks, tokens_all, block_size)
        arrived = lax.ppermute(halves[:, 1].astype(jnp.bfloat16), "dp", pairs)
        other = lax.ppermute(stats, "dp", pairs)
        stats, own, far = merge(stats, other)
        held = (
            halves[:, 0] * own[None, None, :, None]
            + arrived.astype(jnp.float32) * far[None, None, :, None]
        )
        stage *= 2
    column_peak = stats[0]
    stage = 1
    while stage < vocab_count:
        pairs = [(j, j ^ stage) for j in range(vocab_count)]
        stats = merge(stats, lax.ppermute(stats, "vocab", pairs))[0]
        stage *= 2
    teacher_peak, target_total = stats[0], stats[1]
    student_peak, student_total = stats[2], stats[3]
    mapped = jnp.transpose(
        held[0] * jnp.exp(column_peak - teacher_peak)[None, :, None], (1, 0, 2)
    ).reshape(tokens_all, student_cols)

    target_probs = mapped / target_total[:, None]
    student_probs = jnp.exp(student_logits - student_peak[:, None]) / student_total[:, None]
    columns = device_flat * student_cols + jnp.arange(student_cols, dtype=jnp.int32)
    target_hits = (all_targets[:, None] == columns[None, :]).astype(jnp.float32)
    logit_grad = (
        loss_scale
        * (student_probs - (1.0 - hard_weight) * target_probs - hard_weight * target_hits)
    ).astype(jnp.bfloat16)
    partial = lax.dot_general(
        logit_grad, student_head, (((1,), (1,)), ((), ())), preferred_element_type=jnp.float32
    ).astype(jnp.bfloat16)
    shard_count = dp_count * vocab_count
    partial = partial.reshape(shard_count, tokens_all // shard_count, partial.shape[1])
    received = lax.all_to_all(partial, ("dp", "vocab"), split_axis=0, concat_axis=0, tiled=True)
    gradient = jnp.sum(received.astype(jnp.float32), axis=0)
    return gradient.astype(jnp.bfloat16)


def solution(mesh):
    placed = (
        P(("groups", "dp"), None),
        P(None, ("dp", "vocab")),
        P(("dp", "vocab"), None),
        P(("dp", "vocab"), None),
        P(("dp", "vocab"), None, None, None),
        P(("groups", "dp"), None),
        P(None, ("dp", "vocab")),
        P(("groups", "dp")),
    )
    return jax.shard_map(
        on_device,
        mesh=mesh,
        in_specs=placed,
        out_specs=P(("groups", "dp", "vocab"), None),
        check_vma=False,
    )
```

```python
import jax
import jax.numpy as jnp
from jax import lax
from jax.sharding import PartitionSpec as P

hard_weight = 0.25
loss_scale = 64.0


def _code(values):
    return values.astype(jnp.float32).astype(jnp.bfloat16)


def _decode(values):
    return jnp.round(values.astype(jnp.float32)).astype(jnp.int32)


def on_device(
    teacher_hidden,
    teacher_head,
    map_dest,
    map_slot,
    map_weight,
    student_hidden,
    student_head,
    targets,
):
    dp_count = lax.axis_size("dp")
    vocab_count = lax.axis_size("vocab")
    my_dp = lax.axis_index("dp")
    my_vocab = lax.axis_index("vocab")
    block_size = map_weight.shape[2]
    teacher_blocks = map_dest.shape[0]
    fan_count = map_dest.shape[1]
    student_cols = student_head.shape[1]
    student_blocks = student_cols // block_size
    device_flat = my_dp * vocab_count + my_vocab
    item_count = teacher_blocks * fan_count
    local_tokens = teacher_hidden.shape[0]
    teacher_width = teacher_hidden.shape[1]
    student_width = student_hidden.shape[1]

    coded = jnp.concatenate([_code(targets // 256), _code(targets % 256)])
    extra_width = -(-coded.shape[0] // local_tokens)
    extra_width = -(-extra_width // 128) * 128
    coded = jnp.pad(coded, (0, extra_width * local_tokens - coded.shape[0]))
    packed = jnp.concatenate(
        [teacher_hidden, coded.reshape(local_tokens, extra_width)], axis=1
    )
    gathered = lax.all_gather(packed, "dp", axis=0, tiled=True)
    student_all = lax.all_to_all(
        jnp.broadcast_to(student_hidden[None], (dp_count,) + student_hidden.shape),
        "dp", split_axis=0, concat_axis=0, tiled=True,
    ).reshape(dp_count * local_tokens, student_width)
    tokens_all = gathered.shape[0]
    teacher_all = gathered[:, :teacher_width]
    extra_all = gathered[:, teacher_width:].reshape(dp_count, local_tokens * extra_width)
    t_hi = _decode(extra_all[:, :local_tokens])
    t_lo = _decode(extra_all[:, local_tokens : 2 * local_tokens])
    all_targets = (t_hi * 256 + t_lo).reshape(tokens_all)

    teacher_logits = jnp.dot(teacher_all, teacher_head, preferred_element_type=jnp.float32)
    teacher_local_peak = jnp.max(teacher_logits, axis=1)
    teacher_weights = jnp.exp(teacher_logits - teacher_local_peak[:, None]).astype(jnp.bfloat16)
    prob_blocks = teacher_weights.reshape(tokens_all, teacher_blocks, block_size)
    mapped_terms = jnp.einsum(
        "gkc,krcd->krgd", prob_blocks, map_weight, preferred_element_type=jnp.float32
    ).astype(jnp.bfloat16)
    mapped_mass = jnp.sum(mapped_terms.astype(jnp.float32), axis=(0, 1, 3))

    relative = jnp.bitwise_xor(map_dest.reshape(item_count), my_dp)
    row = relative * student_blocks + map_slot.reshape(item_count)
    placement = (
        jnp.arange(dp_count * student_blocks, dtype=jnp.int32)[:, None] == row[None, :]
    ).astype(jnp.bfloat16)
    held = jnp.dot(
        placement,
        mapped_terms.reshape(item_count, tokens_all * block_size),
        preferred_element_type=jnp.float32,
    ).reshape(dp_count, student_blocks, tokens_all, block_size)

    student_logits = jnp.dot(student_all, student_head, preferred_element_type=jnp.float32)
    student_local_peak = jnp.max(student_logits, axis=1)
    student_local_total = jnp.sum(jnp.exp(student_logits - student_local_peak[:, None]), axis=1)

    peak, mass = teacher_local_peak, mapped_mass
    s_peak, s_total = student_local_peak, student_local_total

    def merge(stats, other):
        new_peak = jnp.maximum(stats[0], other[0])
        new_s_peak = jnp.maximum(stats[2], other[2])
        own, far = jnp.exp(stats[0] - new_peak), jnp.exp(other[0] - new_peak)
        s_own, s_far = jnp.exp(stats[2] - new_s_peak), jnp.exp(other[2] - new_s_peak)
        merged = jnp.stack(
            [new_peak, stats[1] * own + other[1] * far, new_s_peak,
             stats[3] * s_own + other[3] * s_far]
        )
        return merged, own, far

    stats = jnp.stack([peak, mass, s_peak, s_total])
    stage = 1
    while stage < dp_count:
        pairs = [(j, j ^ stage) for j in range(dp_count)]
        halves = held.reshape(held.shape[0] // 2, 2, student_blocks, tokens_all, block_size)
        arrived = lax.ppermute(halves[:, 1].astype(jnp.bfloat16), "dp", pairs)
        other = lax.ppermute(stats, "dp", pairs)
        stats, own, far = merge(stats, other)
        held = (
            halves[:, 0] * own[None, None, :, None]
            + arrived.astype(jnp.float32) * far[None, None, :, None]
        )
        stage *= 2
    column_peak = stats[0]
    stage = 1
    while stage < vocab_count:
        pairs = [(j, j ^ stage) for j in range(vocab_count)]
        stats = merge(stats, lax.ppermute(stats, "vocab", pairs))[0]
        stage *= 2
    teacher_peak, target_total = stats[0], stats[1]
    student_peak, student_total = stats[2], stats[3]
    mapped = jnp.transpose(
        held[0] * jnp.exp(column_peak - teacher_peak)[None, :, None], (1, 0, 2)
    ).reshape(tokens_all, student_cols)

    target_probs = mapped / target_total[:, None]
    student_probs = jnp.exp(student_logits - student_peak[:, None]) / student_total[:, None]
    columns = device_flat * student_cols + jnp.arange(student_cols, dtype=jnp.int32)
    target_hits = (all_targets[:, None] == columns[None, :]).astype(jnp.float32)
    logit_grad = (
        loss_scale
        * (student_probs - (1.0 - hard_weight) * target_probs - hard_weight * target_hits)
    ).astype(jnp.bfloat16)
    partial = lax.dot_general(
        logit_grad, student_head, (((1,), (1,)), ((), ())), preferred_element_type=jnp.float32
    ).astype(jnp.bfloat16)
    shard_count = dp_count * vocab_count
    partial = partial.reshape(shard_count, tokens_all // shard_count, partial.shape[1])
    received = lax.all_to_all(partial, ("dp", "vocab"), split_axis=0, concat_axis=0, tiled=True)
    gradient = jnp.sum(received.astype(jnp.float32), axis=0)
    return gradient.astype(jnp.bfloat16)


def solution(mesh):
    placed = (
        P(("groups", "dp"), None),
        P(None, ("dp", "vocab")),
        P(("dp", "vocab"), None),
        P(("dp", "vocab"), None),
        P(("dp", "vocab"), None, None, None),
        P(("groups", "dp"), None),
        P(None, ("dp", "vocab")),
        P(("groups", "dp")),
    )
    return jax.shard_map(
        on_device,
        mesh=mesh,
        in_specs=placed,
        out_specs=P(("groups", "dp", "vocab"), None),
        check_vma=False,
    )
```

```python
import jax
import jax.numpy as jnp
from jax import lax
from jax.sharding import PartitionSpec as P

hard_weight = 0.25
loss_scale = 64.0


def _code(values):
    return values.astype(jnp.float32).astype(jnp.bfloat16)


def _decode(values):
    return jnp.round(values.astype(jnp.float32)).astype(jnp.int32)


def on_device(
    teacher_hidden,
    teacher_head,
    map_dest,
    map_slot,
    map_weight,
    student_hidden,
    student_head,
    targets,
):
    dp_count = lax.axis_size("dp")
    vocab_count = lax.axis_size("vocab")
    my_dp = lax.axis_index("dp")
    my_vocab = lax.axis_index("vocab")
    block_size = map_weight.shape[2]
    teacher_blocks = map_dest.shape[0]
    fan_count = map_dest.shape[1]
    student_cols = student_head.shape[1]
    student_blocks = student_cols // block_size
    device_flat = my_dp * vocab_count + my_vocab
    item_count = teacher_blocks * fan_count
    local_tokens = teacher_hidden.shape[0]
    teacher_width = teacher_hidden.shape[1]
    student_width = student_hidden.shape[1]

    coded = jnp.concatenate([_code(targets // 256), _code(targets % 256)])
    extra_width = -(-coded.shape[0] // local_tokens)
    extra_width = -(-extra_width // 128) * 128
    coded = jnp.pad(coded, (0, extra_width * local_tokens - coded.shape[0]))
    packed = jnp.concatenate(
        [teacher_hidden, coded.reshape(local_tokens, extra_width)], axis=1
    )
    gathered = lax.all_gather(packed, "dp", axis=0, tiled=True)
    student_all = lax.all_to_all(
        jnp.broadcast_to(student_hidden[None], (dp_count,) + student_hidden.shape),
        "dp", split_axis=0, concat_axis=0, tiled=True,
    ).reshape(dp_count * local_tokens, student_width)
    tokens_all = gathered.shape[0]
    teacher_all = gathered[:, :teacher_width]
    extra_all = gathered[:, teacher_width:].reshape(dp_count, local_tokens * extra_width)
    t_hi = _decode(extra_all[:, :local_tokens])
    t_lo = _decode(extra_all[:, local_tokens : 2 * local_tokens])
    all_targets = (t_hi * 256 + t_lo).reshape(tokens_all)

    teacher_logits = jnp.dot(teacher_all, teacher_head, preferred_element_type=jnp.float32)
    teacher_local_peak = jnp.max(teacher_logits, axis=1)
    teacher_weights = jnp.exp(teacher_logits - teacher_local_peak[:, None]).astype(jnp.bfloat16)
    prob_blocks = teacher_weights.reshape(tokens_all, teacher_blocks, block_size)
    mapped_terms = jnp.einsum(
        "gkc,krcd->krgd", prob_blocks, map_weight, preferred_element_type=jnp.float32
    ).astype(jnp.bfloat16)
    mapped_mass = jnp.sum(mapped_terms.astype(jnp.float32), axis=(0, 1, 3))

    relative = jnp.bitwise_xor(map_dest.reshape(item_count), my_dp)
    row = relative * student_blocks + map_slot.reshape(item_count)
    placement = (
        jnp.arange(dp_count * student_blocks, dtype=jnp.int32)[:, None] == row[None, :]
    ).astype(jnp.bfloat16)
    held = jnp.dot(
        placement,
        mapped_terms.reshape(item_count, tokens_all * block_size),
        preferred_element_type=jnp.float32,
    ).reshape(dp_count, student_blocks, tokens_all, block_size)

    student_logits = jnp.dot(student_all, student_head, preferred_element_type=jnp.float32)
    student_local_peak = jnp.max(student_logits, axis=1)
    student_local_total = jnp.sum(jnp.exp(student_logits - student_local_peak[:, None]), axis=1)

    def merge(stats, other):
        new_peak = jnp.maximum(stats[0], other[0])
        new_s_peak = jnp.maximum(stats[2], other[2])
        own, far = jnp.exp(stats[0] - new_peak), jnp.exp(other[0] - new_peak)
        s_own, s_far = jnp.exp(stats[2] - new_s_peak), jnp.exp(other[2] - new_s_peak)
        merged = jnp.stack(
            [new_peak, stats[1] * own + other[1] * far, new_s_peak,
             stats[3] * s_own + other[3] * s_far]
        )
        return merged, own, far

    def to_every_peer(stats):
        spread = jnp.broadcast_to(stats[None], (dp_count,) + stats.shape)
        return lax.all_to_all(spread, "dp", split_axis=0, concat_axis=0, tiled=True)

    teacher_seen = to_every_peer(jnp.stack([teacher_local_peak, mapped_mass]))
    column_peak = jnp.max(teacher_seen[:, 0], axis=0)
    column_scale = jnp.exp(teacher_seen[:, 0] - column_peak[None, :])
    column_mass = jnp.sum(column_scale * teacher_seen[:, 1], axis=0)
    student_seen = to_every_peer(jnp.stack([student_local_peak, student_local_total]))
    column_s_peak = jnp.max(student_seen[:, 0], axis=0)
    column_s_total = jnp.sum(
        jnp.exp(student_seen[:, 0] - column_s_peak[None, :]) * student_seen[:, 1], axis=0
    )

    halves = held.reshape(dp_count // 2, 2, student_blocks, tokens_all, block_size)
    arrived = lax.ppermute(
        halves[:, 1].astype(jnp.bfloat16), "dp", [(j, j ^ 1) for j in range(dp_count)]
    )
    own = jnp.exp(teacher_local_peak - column_peak)
    far = jnp.take(column_scale, jnp.bitwise_xor(my_dp, 1), axis=0)
    held = (
        halves[:, 0] * own[None, None, :, None]
        + arrived.astype(jnp.float32) * far[None, None, :, None]
    )

    def reduce_bits(part, bits, low_first):
        for bit in bits:
            pairs = [(j, j ^ (1 << bit)) for j in range(dp_count)]
            count = part.shape[0] // 2
            if low_first:
                split = part.reshape((count, 2) + part.shape[1:])
                keep, send = split[:, 0], split[:, 1]
            else:
                split = part.reshape((2, count) + part.shape[1:])
                keep, send = split[0], split[1]
            part = keep + lax.ppermute(send.astype(jnp.bfloat16), "dp", pairs).astype(
                jnp.float32
            )
        return part

    bits = list(range(1, dp_count.bit_length() - 1))
    half = tokens_all // 2
    first = reduce_bits(held[:, :, :half], bits, True)
    second = reduce_bits(held[:, :, half:], bits[::-1], False)
    held = jnp.concatenate([first, second], axis=2)

    stats = jnp.stack([column_peak, column_mass, column_s_peak, column_s_total])
    stage = 1
    while stage < vocab_count:
        pairs = [(j, j ^ stage) for j in range(vocab_count)]
        stats = merge(stats, lax.ppermute(stats, "vocab", pairs))[0]
        stage *= 2
    teacher_peak, target_total = stats[0], stats[1]
    student_peak, student_total = stats[2], stats[3]
    mapped = jnp.transpose(
        held[0] * jnp.exp(column_peak - teacher_peak)[None, :, None], (1, 0, 2)
    ).reshape(tokens_all, student_cols)

    target_probs = mapped / target_total[:, None]
    student_probs = jnp.exp(student_logits - student_peak[:, None]) / student_total[:, None]
    columns = device_flat * student_cols + jnp.arange(student_cols, dtype=jnp.int32)
    target_hits = (all_targets[:, None] == columns[None, :]).astype(jnp.float32)
    logit_grad = (
        loss_scale
        * (student_probs - (1.0 - hard_weight) * target_probs - hard_weight * target_hits)
    ).astype(jnp.bfloat16)
    partial = lax.dot_general(
        logit_grad, student_head, (((1,), (1,)), ((), ())), preferred_element_type=jnp.float32
    ).astype(jnp.bfloat16)
    shard_count = dp_count * vocab_count
    partial = partial.reshape(shard_count, tokens_all // shard_count, partial.shape[1])
    received = lax.all_to_all(partial, ("dp", "vocab"), split_axis=0, concat_axis=0, tiled=True)
    gradient = jnp.sum(received.astype(jnp.float32), axis=0)
    return gradient.astype(jnp.bfloat16)


def solution(mesh):
    placed = (
        P(("groups", "dp"), None),
        P(None, ("dp", "vocab")),
        P(("dp", "vocab"), None),
        P(("dp", "vocab"), None),
        P(("dp", "vocab"), None, None, None),
        P(("groups", "dp"), None),
        P(None, ("dp", "vocab")),
        P(("groups", "dp")),
    )
    return jax.shard_map(
        on_device,
        mesh=mesh,
        in_specs=placed,
        out_specs=P(("groups", "dp", "vocab"), None),
        check_vma=False,
    )
```

```python
import jax
import jax.numpy as jnp
from jax import lax
from jax.sharding import PartitionSpec as P

hard_weight = 0.25
loss_scale = 64.0


def _code(values):
    return values.astype(jnp.float32).astype(jnp.bfloat16)


def _decode(values):
    return jnp.round(values.astype(jnp.float32)).astype(jnp.int32)


def on_device(
    teacher_hidden,
    teacher_head,
    map_dest,
    map_slot,
    map_weight,
    student_hidden,
    student_head,
    targets,
):
    dp_count = lax.axis_size("dp")
    vocab_count = lax.axis_size("vocab")
    my_dp = lax.axis_index("dp")
    my_vocab = lax.axis_index("vocab")
    block_size = map_weight.shape[2]
    teacher_blocks = map_dest.shape[0]
    fan_count = map_dest.shape[1]
    student_cols = student_head.shape[1]
    student_blocks = student_cols // block_size
    device_flat = my_dp * vocab_count + my_vocab
    item_count = teacher_blocks * fan_count
    local_tokens = teacher_hidden.shape[0]
    teacher_width = teacher_hidden.shape[1]
    student_width = student_hidden.shape[1]

    coded = jnp.concatenate([_code(targets // 256), _code(targets % 256)])
    extra_width = -(-coded.shape[0] // local_tokens)
    extra_width = -(-extra_width // 128) * 128
    coded = jnp.pad(coded, (0, extra_width * local_tokens - coded.shape[0]))
    packed = jnp.concatenate(
        [teacher_hidden, coded.reshape(local_tokens, extra_width)], axis=1
    )
    gathered = lax.all_gather(packed, "dp", axis=0, tiled=True)
    student_all = lax.all_to_all(
        jnp.broadcast_to(student_hidden[None], (dp_count,) + student_hidden.shape),
        "dp", split_axis=0, concat_axis=0, tiled=True,
    ).reshape(dp_count * local_tokens, student_width)
    tokens_all = gathered.shape[0]
    teacher_all = gathered[:, :teacher_width]
    extra_all = gathered[:, teacher_width:].reshape(dp_count, local_tokens * extra_width)
    t_hi = _decode(extra_all[:, :local_tokens])
    t_lo = _decode(extra_all[:, local_tokens : 2 * local_tokens])
    all_targets = (t_hi * 256 + t_lo).reshape(tokens_all)

    teacher_logits = jnp.dot(teacher_all, teacher_head, preferred_element_type=jnp.float32)
    teacher_local_peak = jnp.max(teacher_logits, axis=1)
    teacher_weights = jnp.exp(teacher_logits - teacher_local_peak[:, None]).astype(jnp.bfloat16)
    prob_blocks = teacher_weights.reshape(tokens_all, teacher_blocks, block_size)
    mapped_terms = jnp.einsum(
        "gkc,krcd->krgd", prob_blocks, map_weight, preferred_element_type=jnp.float32
    ).astype(jnp.bfloat16)
    mapped_mass = jnp.sum(mapped_terms.astype(jnp.float32), axis=(0, 1, 3))

    relative = jnp.bitwise_xor(map_dest.reshape(item_count), my_dp)
    row = relative * student_blocks + map_slot.reshape(item_count)
    placement = (
        jnp.arange(dp_count * student_blocks, dtype=jnp.int32)[:, None] == row[None, :]
    ).astype(jnp.bfloat16)
    held = jnp.dot(
        placement,
        mapped_terms.reshape(item_count, tokens_all * block_size),
        preferred_element_type=jnp.float32,
    ).reshape(dp_count, student_blocks, tokens_all, block_size)

    student_logits = jnp.dot(student_all, student_head, preferred_element_type=jnp.float32)
    student_local_peak = jnp.max(student_logits, axis=1)
    student_local_total = jnp.sum(jnp.exp(student_logits - student_local_peak[:, None]), axis=1)

    peak, mass = teacher_local_peak, mapped_mass
    s_peak, s_total = student_local_peak, student_local_total

    def merge(stats, other):
        new_peak = jnp.maximum(stats[0], other[0])
        new_s_peak = jnp.maximum(stats[2], other[2])
        own, far = jnp.exp(stats[0] - new_peak), jnp.exp(other[0] - new_peak)
        s_own, s_far = jnp.exp(stats[2] - new_s_peak), jnp.exp(other[2] - new_s_peak)
        merged = jnp.stack(
            [new_peak, stats[1] * own + other[1] * far, new_s_peak,
             stats[3] * s_own + other[3] * s_far]
        )
        return merged, own, far

    def code_stats(stats, rows):
        high = lax.reduce_precision(stats, exponent_bits=8, mantissa_bits=7)
        rest = stats - high
        middle = lax.reduce_precision(rest, exponent_bits=8, mantissa_bits=7)
        low = rest - middle
        flat = jnp.concatenate([high, middle, low]).astype(jnp.bfloat16).reshape(-1)
        flat = jnp.pad(flat, (0, rows * block_size - flat.shape[0]))
        return flat.reshape(1, rows, block_size)

    def decode_stats(coded_block):
        flat = coded_block.reshape(-1)[: 12 * tokens_all].astype(jnp.float32)
        pieces = flat.reshape(3, 4, tokens_all)
        return pieces[0] + pieces[1] + pieces[2]

    def exchange(send, stats, pairs):
        rows = send.shape[-2]
        flat = send.reshape((-1, rows, block_size)).astype(jnp.bfloat16)
        payload = jnp.concatenate([flat, code_stats(stats, rows)], axis=0)
        arrived = lax.ppermute(payload, "dp", pairs)
        blocks = arrived[:-1].reshape(send.shape).astype(jnp.float32)
        return blocks, decode_stats(arrived[-1])

    def combine(keep, stats, blocks, other, token_slice):
        merged, own, far = merge(stats, other)
        own, far = own[token_slice], far[token_slice]
        return keep * own[None, None, :, None] + blocks * far[None, None, :, None], merged

    stats = jnp.stack([peak, mass, s_peak, s_total])
    every = slice(None)
    halves = held.reshape(dp_count // 2, 2, student_blocks, tokens_all, block_size)
    blocks, other = exchange(halves[:, 1], stats, [(j, j ^ 1) for j in range(dp_count)])
    held, stats = combine(halves[:, 0], stats, blocks, other, every)

    def reduce_bits(part, stats, bits, low_first, token_slice):
        for bit in bits:
            pairs = [(j, j ^ (1 << bit)) for j in range(dp_count)]
            count = part.shape[0] // 2
            if low_first:
                split = part.reshape((count, 2) + part.shape[1:])
                keep, send = split[:, 0], split[:, 1]
            else:
                split = part.reshape((2, count) + part.shape[1:])
                keep, send = split[0], split[1]
            blocks, other = exchange(send, stats, pairs)
            part, stats = combine(keep, stats, blocks, other, token_slice)
        return part, stats

    bits = list(range(1, dp_count.bit_length() - 1))
    half = tokens_all // 2
    first, stats_first = reduce_bits(held[:, :, :half], stats, bits, True, slice(0, half))
    second, _ = reduce_bits(held[:, :, half:], stats, bits[::-1], False, slice(half, None))
    held = jnp.concatenate([first, second], axis=2)
    stats = stats_first
    column_peak = stats[0]
    stage = 1
    while stage < vocab_count:
        pairs = [(j, j ^ stage) for j in range(vocab_count)]
        stats = merge(stats, lax.ppermute(stats, "vocab", pairs))[0]
        stage *= 2
    teacher_peak, target_total = stats[0], stats[1]
    student_peak, student_total = stats[2], stats[3]
    mapped = jnp.transpose(
        held[0] * jnp.exp(column_peak - teacher_peak)[None, :, None], (1, 0, 2)
    ).reshape(tokens_all, student_cols)

    target_probs = mapped / target_total[:, None]
    student_probs = jnp.exp(student_logits - student_peak[:, None]) / student_total[:, None]
    columns = device_flat * student_cols + jnp.arange(student_cols, dtype=jnp.int32)
    target_hits = (all_targets[:, None] == columns[None, :]).astype(jnp.float32)
    logit_grad = (
        loss_scale
        * (student_probs - (1.0 - hard_weight) * target_probs - hard_weight * target_hits)
    ).astype(jnp.bfloat16)
    partial = lax.dot_general(
        logit_grad, student_head, (((1,), (1,)), ((), ())), preferred_element_type=jnp.float32
    ).astype(jnp.bfloat16)
    shard_count = dp_count * vocab_count
    partial = partial.reshape(shard_count, tokens_all // shard_count, partial.shape[1])
    received = lax.all_to_all(partial, ("dp", "vocab"), split_axis=0, concat_axis=0, tiled=True)
    gradient = jnp.sum(received.astype(jnp.float32), axis=0)
    return gradient.astype(jnp.bfloat16)


def solution(mesh):
    placed = (
        P(("groups", "dp"), None),
        P(None, ("dp", "vocab")),
        P(("dp", "vocab"), None),
        P(("dp", "vocab"), None),
        P(("dp", "vocab"), None, None, None),
        P(("groups", "dp"), None),
        P(None, ("dp", "vocab")),
        P(("groups", "dp")),
    )
    return jax.shard_map(
        on_device,
        mesh=mesh,
        in_specs=placed,
        out_specs=P(("groups", "dp", "vocab"), None),
        check_vma=False,
    )
```

```python
import jax
import jax.numpy as jnp
from jax import lax
from jax.sharding import PartitionSpec as P

hard_weight = 0.25
loss_scale = 64.0


def _code(values):
    return values.astype(jnp.float32).astype(jnp.bfloat16)


def _decode(values):
    return jnp.round(values.astype(jnp.float32)).astype(jnp.int32)


def on_device(
    teacher_hidden,
    teacher_head,
    map_dest,
    map_slot,
    map_weight,
    student_hidden,
    student_head,
    targets,
):
    dp_count = lax.axis_size("dp")
    vocab_count = lax.axis_size("vocab")
    my_dp = lax.axis_index("dp")
    my_vocab = lax.axis_index("vocab")
    block_size = map_weight.shape[2]
    teacher_blocks = map_dest.shape[0]
    fan_count = map_dest.shape[1]
    student_cols = student_head.shape[1]
    student_blocks = student_cols // block_size
    device_flat = my_dp * vocab_count + my_vocab
    item_count = teacher_blocks * fan_count
    local_tokens = teacher_hidden.shape[0]
    teacher_width = teacher_hidden.shape[1]
    student_width = student_hidden.shape[1]

    coded = jnp.concatenate([_code(targets // 256), _code(targets % 256)])
    extra_width = -(-coded.shape[0] // local_tokens)
    extra_width = -(-extra_width // 128) * 128
    coded = jnp.pad(coded, (0, extra_width * local_tokens - coded.shape[0]))
    packed = jnp.concatenate(
        [teacher_hidden, coded.reshape(local_tokens, extra_width)], axis=1
    )
    gathered = lax.all_gather(packed, "dp", axis=0, tiled=True)
    student_all = lax.all_to_all(
        jnp.broadcast_to(student_hidden[None], (dp_count,) + student_hidden.shape),
        "dp", split_axis=0, concat_axis=0, tiled=True,
    ).reshape(dp_count * local_tokens, student_width)
    tokens_all = gathered.shape[0]
    teacher_all = gathered[:, :teacher_width]
    extra_all = gathered[:, teacher_width:].reshape(dp_count, local_tokens * extra_width)
    t_hi = _decode(extra_all[:, :local_tokens])
    t_lo = _decode(extra_all[:, local_tokens : 2 * local_tokens])
    all_targets = (t_hi * 256 + t_lo).reshape(tokens_all)

    teacher_logits = jnp.dot(teacher_all, teacher_head, preferred_element_type=jnp.float32)
    teacher_local_peak = jnp.max(teacher_logits, axis=1)
    teacher_weights = jnp.exp(teacher_logits - teacher_local_peak[:, None]).astype(jnp.bfloat16)
    prob_blocks = teacher_weights.reshape(tokens_all, teacher_blocks, block_size)
    mapped_terms = jnp.einsum(
        "gkc,krcd->krgd", prob_blocks, map_weight, preferred_element_type=jnp.float32
    ).astype(jnp.bfloat16)
    mapped_mass = jnp.sum(mapped_terms.astype(jnp.float32), axis=(0, 1, 3))

    relative = jnp.bitwise_xor(map_dest.reshape(item_count), my_dp)
    row = relative * student_blocks + map_slot.reshape(item_count)
    placement = (
        jnp.arange(dp_count * student_blocks, dtype=jnp.int32)[:, None] == row[None, :]
    ).astype(jnp.bfloat16)
    held = jnp.dot(
        placement,
        mapped_terms.reshape(item_count, tokens_all * block_size),
        preferred_element_type=jnp.float32,
    ).reshape(dp_count, student_blocks, tokens_all, block_size)

    student_logits = jnp.dot(student_all, student_head, preferred_element_type=jnp.float32)
    student_local_peak = jnp.max(student_logits, axis=1)
    student_local_total = jnp.sum(jnp.exp(student_logits - student_local_peak[:, None]), axis=1)

    peak, mass = teacher_local_peak, mapped_mass
    s_peak, s_total = student_local_peak, student_local_total

    def merge(stats, other):
        new_peak = jnp.maximum(stats[0], other[0])
        own, far = jnp.exp(stats[0] - new_peak), jnp.exp(other[0] - new_peak)
        return jnp.stack([new_peak, stats[1] * own + other[1] * far]), own, far

    teacher_stats = jnp.stack([peak, mass])
    student_stats = jnp.stack([s_peak, s_total])
    stage = 1
    while stage < dp_count:
        pairs = [(j, j ^ stage) for j in range(dp_count)]
        halves = held.reshape(held.shape[0] // 2, 2, student_blocks, tokens_all, block_size)
        arrived = lax.ppermute(halves[:, 1].astype(jnp.bfloat16), "dp", pairs)
        teacher_stats, own, far = merge(teacher_stats, lax.ppermute(teacher_stats, "dp", pairs))
        student_stats = merge(student_stats, lax.ppermute(student_stats, "dp", pairs))[0]
        held = (
            halves[:, 0] * own[None, None, :, None]
            + arrived.astype(jnp.float32) * far[None, None, :, None]
        )
        stage *= 2
    column_peak = teacher_stats[0]
    stage = 1
    while stage < vocab_count:
        pairs = [(j, j ^ stage) for j in range(vocab_count)]
        teacher_stats = merge(teacher_stats, lax.ppermute(teacher_stats, "vocab", pairs))[0]
        student_stats = merge(student_stats, lax.ppermute(student_stats, "vocab", pairs))[0]
        stage *= 2
    teacher_peak, target_total = teacher_stats[0], teacher_stats[1]
    student_peak, student_total = student_stats[0], student_stats[1]
    mapped = jnp.transpose(
        held[0] * jnp.exp(column_peak - teacher_peak)[None, :, None], (1, 0, 2)
    ).reshape(tokens_all, student_cols)

    target_probs = mapped / target_total[:, None]
    student_probs = jnp.exp(student_logits - student_peak[:, None]) / student_total[:, None]
    columns = device_flat * student_cols + jnp.arange(student_cols, dtype=jnp.int32)
    target_hits = (all_targets[:, None] == columns[None, :]).astype(jnp.float32)
    logit_grad = (
        loss_scale
        * (student_probs - (1.0 - hard_weight) * target_probs - hard_weight * target_hits)
    ).astype(jnp.bfloat16)
    partial = lax.dot_general(
        logit_grad, student_head, (((1,), (1,)), ((), ())), preferred_element_type=jnp.float32
    ).astype(jnp.bfloat16)
    shard_count = dp_count * vocab_count
    partial = partial.reshape(shard_count, tokens_all // shard_count, partial.shape[1])
    received = lax.all_to_all(partial, ("dp", "vocab"), split_axis=0, concat_axis=0, tiled=True)
    gradient = jnp.sum(received.astype(jnp.float32), axis=0)
    return gradient.astype(jnp.bfloat16)


def solution(mesh):
    placed = (
        P(("groups", "dp"), None),
        P(None, ("dp", "vocab")),
        P(("dp", "vocab"), None),
        P(("dp", "vocab"), None),
        P(("dp", "vocab"), None, None, None),
        P(("groups", "dp"), None),
        P(None, ("dp", "vocab")),
        P(("groups", "dp")),
    )
    return jax.shard_map(
        on_device,
        mesh=mesh,
        in_specs=placed,
        out_specs=P(("groups", "dp", "vocab"), None),
        check_vma=False,
    )
```

```python
import jax
import jax.numpy as jnp
from jax import lax
from jax.sharding import PartitionSpec as P

hard_weight = 0.25
loss_scale = 64.0


def _code(values):
    return values.astype(jnp.float32).astype(jnp.bfloat16)


def _decode(values):
    return jnp.round(values.astype(jnp.float32)).astype(jnp.int32)


def on_device(
    teacher_hidden,
    teacher_head,
    map_dest,
    map_slot,
    map_weight,
    student_hidden,
    student_head,
    targets,
):
    dp_count = lax.axis_size("dp")
    vocab_count = lax.axis_size("vocab")
    my_dp = lax.axis_index("dp")
    my_vocab = lax.axis_index("vocab")
    block_size = map_weight.shape[2]
    teacher_blocks = map_dest.shape[0]
    fan_count = map_dest.shape[1]
    student_cols = student_head.shape[1]
    student_blocks = student_cols // block_size
    device_flat = my_dp * vocab_count + my_vocab
    item_count = teacher_blocks * fan_count
    local_tokens = teacher_hidden.shape[0]
    teacher_width = teacher_hidden.shape[1]
    student_width = student_hidden.shape[1]

    coded = jnp.concatenate([_code(targets // 256), _code(targets % 256)])
    extra_width = -(-coded.shape[0] // local_tokens)
    extra_width = -(-extra_width // 128) * 128
    coded = jnp.pad(coded, (0, extra_width * local_tokens - coded.shape[0]))
    packed = jnp.concatenate(
        [teacher_hidden, coded.reshape(local_tokens, extra_width)], axis=1
    )
    gathered = lax.all_gather(packed, "dp", axis=0, tiled=True)
    student_all = lax.all_to_all(
        jnp.broadcast_to(student_hidden[None], (dp_count,) + student_hidden.shape),
        "dp", split_axis=0, concat_axis=0, tiled=True,
    ).reshape(dp_count * local_tokens, student_width)
    tokens_all = gathered.shape[0]
    teacher_all = gathered[:, :teacher_width]
    extra_all = gathered[:, teacher_width:].reshape(dp_count, local_tokens * extra_width)
    t_hi = _decode(extra_all[:, :local_tokens])
    t_lo = _decode(extra_all[:, local_tokens : 2 * local_tokens])
    all_targets = (t_hi * 256 + t_lo).reshape(tokens_all)

    teacher_logits = jnp.dot(teacher_all, teacher_head, preferred_element_type=jnp.float32)
    teacher_local_peak = jnp.max(teacher_logits, axis=1)
    teacher_weights = jnp.exp(teacher_logits - teacher_local_peak[:, None]).astype(jnp.bfloat16)
    prob_blocks = teacher_weights.reshape(tokens_all, teacher_blocks, block_size)
    mapped_terms = jnp.einsum(
        "gkc,krcd->krgd", prob_blocks, map_weight, preferred_element_type=jnp.float32
    ).astype(jnp.bfloat16)
    mapped_mass = jnp.sum(mapped_terms.astype(jnp.float32), axis=(0, 1, 3))

    relative = jnp.bitwise_xor(map_dest.reshape(item_count), my_dp)
    row = relative * student_blocks + map_slot.reshape(item_count)
    placement = (
        jnp.arange(dp_count * student_blocks, dtype=jnp.int32)[:, None] == row[None, :]
    ).astype(jnp.bfloat16)
    held = jnp.dot(
        placement,
        mapped_terms.reshape(item_count, tokens_all * block_size),
        preferred_element_type=jnp.float32,
    ).reshape(dp_count, student_blocks, tokens_all, block_size)

    student_logits = jnp.dot(student_all, student_head, preferred_element_type=jnp.float32)
    student_local_peak = jnp.max(student_logits, axis=1)
    student_local_total = jnp.sum(jnp.exp(student_logits - student_local_peak[:, None]), axis=1)

    peak, mass = teacher_local_peak, mapped_mass
    s_peak, s_total = student_local_peak, student_local_total

    def merge(stats, other):
        new_peak = jnp.maximum(stats[0], other[0])
        own, far = jnp.exp(stats[0] - new_peak), jnp.exp(other[0] - new_peak)
        return jnp.stack([new_peak, stats[1] * own + other[1] * far]), own, far

    teacher_stats = jnp.stack([peak, mass])
    student_stats = jnp.stack([s_peak, s_total])
    stage = 1
    while stage < dp_count:
        pairs = [(j, j ^ stage) for j in range(dp_count)]
        teacher_stats = merge(teacher_stats, lax.ppermute(teacher_stats, "dp", pairs))[0]
        student_stats = merge(student_stats, lax.ppermute(student_stats, "dp", pairs))[0]
        stage *= 2
    column_peak = teacher_stats[0]
    held = held * jnp.exp(teacher_local_peak - column_peak)[None, None, :, None]

    def reduce_bits(part, bits, low_first):
        for bit in bits:
            pairs = [(j, j ^ (1 << bit)) for j in range(dp_count)]
            count = part.shape[0] // 2
            if low_first:
                split = part.reshape((count, 2) + part.shape[1:])
                keep, send = split[:, 0], split[:, 1]
            else:
                split = part.reshape((2, count) + part.shape[1:])
                keep, send = split[0], split[1]
            part = keep + lax.ppermute(send.astype(jnp.bfloat16), "dp", pairs).astype(
                jnp.float32
            )
        return part

    held = reduce_bits(held, [0], True)
    bits = list(range(1, dp_count.bit_length() - 1))
    half = tokens_all // 2
    first = reduce_bits(held[:, :, :half], bits, True)
    second = reduce_bits(held[:, :, half:], bits[::-1], False)
    held = jnp.concatenate([first, second], axis=2)

    stage = 1
    while stage < vocab_count:
        pairs = [(j, j ^ stage) for j in range(vocab_count)]
        teacher_stats = merge(teacher_stats, lax.ppermute(teacher_stats, "vocab", pairs))[0]
        student_stats = merge(student_stats, lax.ppermute(student_stats, "vocab", pairs))[0]
        stage *= 2
    teacher_peak, target_total = teacher_stats[0], teacher_stats[1]
    student_peak, student_total = student_stats[0], student_stats[1]
    mapped = jnp.transpose(
        held[0] * jnp.exp(column_peak - teacher_peak)[None, :, None], (1, 0, 2)
    ).reshape(tokens_all, student_cols)

    target_probs = mapped / target_total[:, None]
    student_probs = jnp.exp(student_logits - student_peak[:, None]) / student_total[:, None]
    columns = device_flat * student_cols + jnp.arange(student_cols, dtype=jnp.int32)
    target_hits = (all_targets[:, None] == columns[None, :]).astype(jnp.float32)
    logit_grad = (
        loss_scale
        * (student_probs - (1.0 - hard_weight) * target_probs - hard_weight * target_hits)
    ).astype(jnp.bfloat16)
    partial = lax.dot_general(
        logit_grad, student_head, (((1,), (1,)), ((), ())), preferred_element_type=jnp.float32
    ).astype(jnp.bfloat16)
    shard_count = dp_count * vocab_count
    partial = partial.reshape(shard_count, tokens_all // shard_count, partial.shape[1])
    received = lax.all_to_all(partial, ("dp", "vocab"), split_axis=0, concat_axis=0, tiled=True)
    gradient = jnp.sum(received.astype(jnp.float32), axis=0)
    return gradient.astype(jnp.bfloat16)


def solution(mesh):
    placed = (
        P(("groups", "dp"), None),
        P(None, ("dp", "vocab")),
        P(("dp", "vocab"), None),
        P(("dp", "vocab"), None),
        P(("dp", "vocab"), None, None, None),
        P(("groups", "dp"), None),
        P(None, ("dp", "vocab")),
        P(("groups", "dp")),
    )
    return jax.shard_map(
        on_device,
        mesh=mesh,
        in_specs=placed,
        out_specs=P(("groups", "dp", "vocab"), None),
        check_vma=False,
    )
```

```python
import jax
import jax.numpy as jnp
from jax import lax
from jax.sharding import PartitionSpec as P

hard_weight = 0.25
loss_scale = 64.0


def _code(values):
    return values.astype(jnp.float32).astype(jnp.bfloat16)


def _decode(values):
    return jnp.round(values.astype(jnp.float32)).astype(jnp.int32)


def on_device(
    teacher_hidden,
    teacher_head,
    map_dest,
    map_slot,
    map_weight,
    student_hidden,
    student_head,
    targets,
):
    dp_count = lax.axis_size("dp")
    vocab_count = lax.axis_size("vocab")
    my_dp = lax.axis_index("dp")
    my_vocab = lax.axis_index("vocab")
    block_size = map_weight.shape[2]
    teacher_blocks = map_dest.shape[0]
    fan_count = map_dest.shape[1]
    student_cols = student_head.shape[1]
    student_blocks = student_cols // block_size
    device_flat = my_dp * vocab_count + my_vocab
    item_count = teacher_blocks * fan_count
    local_tokens = teacher_hidden.shape[0]
    teacher_width = teacher_hidden.shape[1]
    student_width = student_hidden.shape[1]

    coded = jnp.concatenate([_code(targets // 256), _code(targets % 256)])
    extra_width = -(-coded.shape[0] // local_tokens)
    extra_width = -(-extra_width // 128) * 128
    coded = jnp.pad(coded, (0, extra_width * local_tokens - coded.shape[0]))
    packed = jnp.concatenate(
        [teacher_hidden, student_hidden, coded.reshape(local_tokens, extra_width)], axis=1
    )
    gathered = lax.all_gather(packed, "dp", axis=0, tiled=True)
    tokens_all = gathered.shape[0]
    teacher_all = gathered[:, :teacher_width]
    student_all = gathered[:, teacher_width : teacher_width + student_width]
    extra_all = gathered[:, teacher_width + student_width :].reshape(
        dp_count, local_tokens * extra_width
    )
    t_hi = _decode(extra_all[:, :local_tokens])
    t_lo = _decode(extra_all[:, local_tokens : 2 * local_tokens])
    all_targets = (t_hi * 256 + t_lo).reshape(tokens_all)

    teacher_logits = jnp.dot(teacher_all, teacher_head, preferred_element_type=jnp.float32)
    teacher_local_peak = jnp.max(teacher_logits, axis=1)
    teacher_weights = jnp.exp(teacher_logits - teacher_local_peak[:, None]).astype(jnp.bfloat16)
    prob_blocks = teacher_weights.reshape(tokens_all, teacher_blocks, block_size)
    mapped_terms = jnp.einsum(
        "gkc,krcd->krgd", prob_blocks, map_weight, preferred_element_type=jnp.float32
    ).astype(jnp.bfloat16)
    mapped_mass = jnp.sum(mapped_terms.astype(jnp.float32), axis=(0, 1, 3))

    relative = jnp.bitwise_xor(map_dest.reshape(item_count), my_dp)
    row = relative * student_blocks + map_slot.reshape(item_count)
    placement = (
        jnp.arange(dp_count * student_blocks, dtype=jnp.int32)[:, None] == row[None, :]
    ).astype(jnp.bfloat16)
    held = jnp.dot(
        placement,
        mapped_terms.reshape(item_count, tokens_all * block_size),
        preferred_element_type=jnp.float32,
    ).reshape(dp_count, student_blocks, tokens_all, block_size)

    student_logits = jnp.dot(student_all, student_head, preferred_element_type=jnp.float32)
    student_local_peak = jnp.max(student_logits, axis=1)
    student_local_total = jnp.sum(jnp.exp(student_logits - student_local_peak[:, None]), axis=1)

    peak, mass = teacher_local_peak, mapped_mass
    s_peak, s_total = student_local_peak, student_local_total

    def merge(stats, other):
        new_peak = jnp.maximum(stats[0], other[0])
        own, far = jnp.exp(stats[0] - new_peak), jnp.exp(other[0] - new_peak)
        return jnp.stack([new_peak, stats[1] * own + other[1] * far]), own, far

    teacher_stats = jnp.stack([peak, mass])
    student_stats = jnp.stack([s_peak, s_total])
    stage = 1
    while stage < dp_count:
        pairs = [(j, j ^ stage) for j in range(dp_count)]
        teacher_stats = merge(teacher_stats, lax.ppermute(teacher_stats, "dp", pairs))[0]
        student_stats = merge(student_stats, lax.ppermute(student_stats, "dp", pairs))[0]
        stage *= 2
    column_peak = teacher_stats[0]
    held = held * jnp.exp(teacher_local_peak - column_peak)[None, None, :, None]

    def reduce_bits(part, bits, low_first):
        for bit in bits:
            pairs = [(j, j ^ (1 << bit)) for j in range(dp_count)]
            count = part.shape[0] // 2
            if low_first:
                split = part.reshape((count, 2) + part.shape[1:])
                keep, send = split[:, 0], split[:, 1]
            else:
                split = part.reshape((2, count) + part.shape[1:])
                keep, send = split[0], split[1]
            part = keep + lax.ppermute(send.astype(jnp.bfloat16), "dp", pairs).astype(
                jnp.float32
            )
        return part

    held = reduce_bits(held, [0], True)
    bits = list(range(1, dp_count.bit_length() - 1))
    half = tokens_all // 2
    first = reduce_bits(held[:, :, :half], bits, True)
    second = reduce_bits(held[:, :, half:], bits[::-1], False)
    held = jnp.concatenate([first, second], axis=2)

    stage = 1
    while stage < vocab_count:
        pairs = [(j, j ^ stage) for j in range(vocab_count)]
        teacher_stats = merge(teacher_stats, lax.ppermute(teacher_stats, "vocab", pairs))[0]
        student_stats = merge(student_stats, lax.ppermute(student_stats, "vocab", pairs))[0]
        stage *= 2
    teacher_peak, target_total = teacher_stats[0], teacher_stats[1]
    student_peak, student_total = student_stats[0], student_stats[1]
    mapped = jnp.transpose(
        held[0] * jnp.exp(column_peak - teacher_peak)[None, :, None], (1, 0, 2)
    ).reshape(tokens_all, student_cols)

    target_probs = mapped / target_total[:, None]
    student_probs = jnp.exp(student_logits - student_peak[:, None]) / student_total[:, None]
    columns = device_flat * student_cols + jnp.arange(student_cols, dtype=jnp.int32)
    target_hits = (all_targets[:, None] == columns[None, :]).astype(jnp.float32)
    logit_grad = (
        loss_scale
        * (student_probs - (1.0 - hard_weight) * target_probs - hard_weight * target_hits)
    ).astype(jnp.bfloat16)
    partial = lax.dot_general(
        logit_grad, student_head, (((1,), (1,)), ((), ())), preferred_element_type=jnp.float32
    ).astype(jnp.bfloat16)
    shard_count = dp_count * vocab_count
    partial = partial.reshape(shard_count, tokens_all // shard_count, partial.shape[1])
    received = lax.all_to_all(partial, ("dp", "vocab"), split_axis=0, concat_axis=0, tiled=True)
    gradient = jnp.sum(received.astype(jnp.float32), axis=0)
    return gradient.astype(jnp.bfloat16)


def solution(mesh):
    placed = (
        P(("groups", "dp"), None),
        P(None, ("dp", "vocab")),
        P(("dp", "vocab"), None),
        P(("dp", "vocab"), None),
        P(("dp", "vocab"), None, None, None),
        P(("groups", "dp"), None),
        P(None, ("dp", "vocab")),
        P(("groups", "dp")),
    )
    return jax.shard_map(
        on_device,
        mesh=mesh,
        in_specs=placed,
        out_specs=P(("groups", "dp", "vocab"), None),
        check_vma=False,
    )
```

```python
import jax
import jax.numpy as jnp
from jax import lax
from jax.sharding import PartitionSpec as P

hard_weight = 0.25
loss_scale = 64.0


def _code(values):
    return values.astype(jnp.float32).astype(jnp.bfloat16)


def _decode(values):
    return jnp.round(values.astype(jnp.float32)).astype(jnp.int32)


def on_device(
    teacher_hidden,
    teacher_head,
    map_dest,
    map_slot,
    map_weight,
    student_hidden,
    student_head,
    targets,
):
    dp_count = lax.axis_size("dp")
    vocab_count = lax.axis_size("vocab")
    my_dp = lax.axis_index("dp")
    my_vocab = lax.axis_index("vocab")
    block_size = map_weight.shape[2]
    teacher_blocks = map_dest.shape[0]
    fan_count = map_dest.shape[1]
    student_cols = student_head.shape[1]
    student_blocks = student_cols // block_size
    device_flat = my_dp * vocab_count + my_vocab
    item_count = teacher_blocks * fan_count
    local_tokens = teacher_hidden.shape[0]
    teacher_width = teacher_hidden.shape[1]
    student_width = student_hidden.shape[1]

    coded = jnp.concatenate([_code(targets // 256), _code(targets % 256)])
    extra_width = -(-coded.shape[0] // local_tokens)
    extra_width = -(-extra_width // 128) * 128
    coded = jnp.pad(coded, (0, extra_width * local_tokens - coded.shape[0]))
    packed = jnp.concatenate(
        [teacher_hidden, coded.reshape(local_tokens, extra_width)], axis=1
    )
    gathered = lax.all_gather(packed, "dp", axis=0, tiled=True)
    student_all = lax.all_to_all(
        jnp.broadcast_to(student_hidden[None], (dp_count,) + student_hidden.shape),
        "dp", split_axis=0, concat_axis=0, tiled=True,
    ).reshape(dp_count * local_tokens, student_width)
    tokens_all = gathered.shape[0]
    teacher_all = gathered[:, :teacher_width]
    extra_all = gathered[:, teacher_width:].reshape(dp_count, local_tokens * extra_width)
    t_hi = _decode(extra_all[:, :local_tokens])
    t_lo = _decode(extra_all[:, local_tokens : 2 * local_tokens])
    all_targets = (t_hi * 256 + t_lo).reshape(tokens_all)

    teacher_logits = jnp.dot(teacher_all, teacher_head, preferred_element_type=jnp.float32)
    teacher_local_peak = jnp.max(teacher_logits, axis=1)
    teacher_weights = jnp.exp(teacher_logits - teacher_local_peak[:, None]).astype(jnp.bfloat16)
    prob_blocks = teacher_weights.reshape(tokens_all, teacher_blocks, block_size)
    mapped_terms = jnp.einsum(
        "gkc,krcd->krgd", prob_blocks, map_weight, preferred_element_type=jnp.float32
    ).astype(jnp.bfloat16)
    mapped_mass = jnp.sum(mapped_terms.astype(jnp.float32), axis=(0, 1, 3))

    relative = jnp.bitwise_xor(map_dest.reshape(item_count), my_dp)
    row = relative * student_blocks + map_slot.reshape(item_count)
    placement = (
        jnp.arange(dp_count * student_blocks, dtype=jnp.int32)[:, None] == row[None, :]
    ).astype(jnp.bfloat16)
    held = jnp.dot(
        placement,
        mapped_terms.reshape(item_count, tokens_all * block_size),
        preferred_element_type=jnp.float32,
    ).reshape(dp_count, student_blocks, tokens_all, block_size)

    peak, mass = teacher_local_peak, mapped_mass

    def merge(stats, other):
        new_peak = jnp.maximum(stats[0], other[0])
        own, far = jnp.exp(stats[0] - new_peak), jnp.exp(other[0] - new_peak)
        return jnp.stack([new_peak, stats[1] * own + other[1] * far]), own, far

    teacher_stats = jnp.stack([peak, mass])
    stage = 1
    while stage < dp_count:
        pairs = [(j, j ^ stage) for j in range(dp_count)]
        teacher_stats = merge(teacher_stats, lax.ppermute(teacher_stats, "dp", pairs))[0]
        stage *= 2
    column_peak = teacher_stats[0]
    held = held * jnp.exp(teacher_local_peak - column_peak)[None, None, :, None]

    def reduce_bits(part, bits, low_first):
        for bit in bits:
            pairs = [(j, j ^ (1 << bit)) for j in range(dp_count)]
            count = part.shape[0] // 2
            if low_first:
                split = part.reshape((count, 2) + part.shape[1:])
                keep, send = split[:, 0], split[:, 1]
            else:
                split = part.reshape((2, count) + part.shape[1:])
                keep, send = split[0], split[1]
            part = keep + lax.ppermute(send.astype(jnp.bfloat16), "dp", pairs).astype(
                jnp.float32
            )
        return part

    held = reduce_bits(held, [0], True)
    held, student_all = lax.optimization_barrier((held, student_all))
    student_logits = jnp.dot(student_all, student_head, preferred_element_type=jnp.float32)
    student_local_peak = jnp.max(student_logits, axis=1)
    student_local_total = jnp.sum(jnp.exp(student_logits - student_local_peak[:, None]), axis=1)
    student_stats = jnp.stack([student_local_peak, student_local_total])
    stage = 1
    while stage < dp_count:
        pairs = [(j, j ^ stage) for j in range(dp_count)]
        student_stats = merge(student_stats, lax.ppermute(student_stats, "dp", pairs))[0]
        stage *= 2
    bits = list(range(1, dp_count.bit_length() - 1))
    half = tokens_all // 2
    first = reduce_bits(held[:, :, :half], bits, True)
    second = reduce_bits(held[:, :, half:], bits[::-1], False)
    held = jnp.concatenate([first, second], axis=2)

    stage = 1
    while stage < vocab_count:
        pairs = [(j, j ^ stage) for j in range(vocab_count)]
        teacher_stats = merge(teacher_stats, lax.ppermute(teacher_stats, "vocab", pairs))[0]
        student_stats = merge(student_stats, lax.ppermute(student_stats, "vocab", pairs))[0]
        stage *= 2
    teacher_peak, target_total = teacher_stats[0], teacher_stats[1]
    student_peak, student_total = student_stats[0], student_stats[1]
    mapped = jnp.transpose(
        held[0] * jnp.exp(column_peak - teacher_peak)[None, :, None], (1, 0, 2)
    ).reshape(tokens_all, student_cols)

    target_probs = mapped / target_total[:, None]
    student_probs = jnp.exp(student_logits - student_peak[:, None]) / student_total[:, None]
    columns = device_flat * student_cols + jnp.arange(student_cols, dtype=jnp.int32)
    target_hits = (all_targets[:, None] == columns[None, :]).astype(jnp.float32)
    logit_grad = (
        loss_scale
        * (student_probs - (1.0 - hard_weight) * target_probs - hard_weight * target_hits)
    ).astype(jnp.bfloat16)
    partial = lax.dot_general(
        logit_grad, student_head, (((1,), (1,)), ((), ())), preferred_element_type=jnp.float32
    ).astype(jnp.bfloat16)
    shard_count = dp_count * vocab_count
    partial = partial.reshape(shard_count, tokens_all // shard_count, partial.shape[1])
    received = lax.all_to_all(partial, ("dp", "vocab"), split_axis=0, concat_axis=0, tiled=True)
    gradient = jnp.sum(received.astype(jnp.float32), axis=0)
    return gradient.astype(jnp.bfloat16)


def solution(mesh):
    placed = (
        P(("groups", "dp"), None),
        P(None, ("dp", "vocab")),
        P(("dp", "vocab"), None),
        P(("dp", "vocab"), None),
        P(("dp", "vocab"), None, None, None),
        P(("groups", "dp"), None),
        P(None, ("dp", "vocab")),
        P(("groups", "dp")),
    )
    return jax.shard_map(
        on_device,
        mesh=mesh,
        in_specs=placed,
        out_specs=P(("groups", "dp", "vocab"), None),
        check_vma=False,
    )
```

```python
import jax
import jax.numpy as jnp
from jax import lax
from jax.sharding import PartitionSpec as P

hard_weight = 0.25
loss_scale = 64.0


def _code(values):
    return values.astype(jnp.float32).astype(jnp.bfloat16)


def _decode(values):
    return jnp.round(values.astype(jnp.float32)).astype(jnp.int32)


def on_device(
    teacher_hidden,
    teacher_head,
    map_dest,
    map_slot,
    map_weight,
    student_hidden,
    student_head,
    targets,
):
    dp_count = lax.axis_size("dp")
    vocab_count = lax.axis_size("vocab")
    my_dp = lax.axis_index("dp")
    my_vocab = lax.axis_index("vocab")
    block_size = map_weight.shape[2]
    teacher_blocks = map_dest.shape[0]
    fan_count = map_dest.shape[1]
    student_cols = student_head.shape[1]
    student_blocks = student_cols // block_size
    device_flat = my_dp * vocab_count + my_vocab
    item_count = teacher_blocks * fan_count
    local_tokens = teacher_hidden.shape[0]
    teacher_width = teacher_hidden.shape[1]
    student_width = student_hidden.shape[1]

    coded = jnp.concatenate([_code(targets // 256), _code(targets % 256)])
    extra_width = -(-coded.shape[0] // local_tokens)
    extra_width = -(-extra_width // 128) * 128
    coded = jnp.pad(coded, (0, extra_width * local_tokens - coded.shape[0]))
    packed = jnp.concatenate(
        [teacher_hidden, coded.reshape(local_tokens, extra_width)], axis=1
    )
    gathered = lax.all_gather(packed, "dp", axis=0, tiled=True)
    student_all = lax.all_to_all(
        jnp.broadcast_to(student_hidden[None], (dp_count,) + student_hidden.shape),
        "dp", split_axis=0, concat_axis=0, tiled=True,
    ).reshape(dp_count * local_tokens, student_width)
    tokens_all = gathered.shape[0]
    teacher_all = gathered[:, :teacher_width]
    extra_all = gathered[:, teacher_width:].reshape(dp_count, local_tokens * extra_width)
    t_hi = _decode(extra_all[:, :local_tokens])
    t_lo = _decode(extra_all[:, local_tokens : 2 * local_tokens])
    all_targets = (t_hi * 256 + t_lo).reshape(tokens_all)

    teacher_logits = jnp.dot(teacher_all, teacher_head, preferred_element_type=jnp.float32)
    teacher_local_peak = jnp.max(teacher_logits, axis=1)
    teacher_weights = jnp.exp(teacher_logits - teacher_local_peak[:, None]).astype(jnp.bfloat16)
    prob_blocks = teacher_weights.reshape(tokens_all, teacher_blocks, block_size)
    mapped_terms = jnp.einsum(
        "gkc,krcd->krgd", prob_blocks, map_weight, preferred_element_type=jnp.float32
    ).astype(jnp.bfloat16)
    mapped_mass = jnp.sum(mapped_terms.astype(jnp.float32), axis=(0, 1, 3))

    relative = jnp.bitwise_xor(map_dest.reshape(item_count), my_dp)
    row = relative * student_blocks + map_slot.reshape(item_count)
    placement = (
        jnp.arange(dp_count * student_blocks, dtype=jnp.int32)[:, None] == row[None, :]
    ).astype(jnp.bfloat16)
    held = jnp.dot(
        placement,
        mapped_terms.reshape(item_count, tokens_all * block_size),
        preferred_element_type=jnp.float32,
    ).reshape(dp_count, student_blocks, tokens_all, block_size)

    student_logits = jnp.dot(student_all, student_head, preferred_element_type=jnp.float32)
    student_local_peak = jnp.max(student_logits, axis=1)
    student_local_total = jnp.sum(jnp.exp(student_logits - student_local_peak[:, None]), axis=1)

    peak, mass = teacher_local_peak, mapped_mass
    s_peak, s_total = student_local_peak, student_local_total

    def merge(stats, other):
        new_peak = jnp.maximum(stats[0], other[0])
        own, far = jnp.exp(stats[0] - new_peak), jnp.exp(other[0] - new_peak)
        return jnp.stack([new_peak, stats[1] * own + other[1] * far]), own, far

    teacher_stats = jnp.stack([peak, mass])
    student_stats = jnp.stack([s_peak, s_total])
    stage = 1
    while stage < dp_count:
        pairs = [(j, j ^ stage) for j in range(dp_count)]
        teacher_stats = merge(teacher_stats, lax.ppermute(teacher_stats, "dp", pairs))[0]
        student_stats = merge(student_stats, lax.ppermute(student_stats, "dp", pairs))[0]
        stage *= 2
    column_peak = teacher_stats[0]
    to_column = jnp.exp(teacher_local_peak - column_peak)[None, None, :, None]

    def reduce_bits(part, bits, low_first):
        for bit in bits:
            pairs = [(j, j ^ (1 << bit)) for j in range(dp_count)]
            count = part.shape[0] // 2
            if low_first:
                split = part.reshape((count, 2) + part.shape[1:])
                keep, send = split[:, 0], split[:, 1]
            else:
                split = part.reshape((2, count) + part.shape[1:])
                keep, send = split[0], split[1]
            part = keep + lax.ppermute(send.astype(jnp.bfloat16), "dp", pairs).astype(
                jnp.float32
            )
        return part

    pair = held.reshape((held.shape[0] // 2, 2) + held.shape[1:])
    arrived = lax.ppermute(
        (pair[:, 1] * to_column).astype(jnp.bfloat16), "dp", [(j, j ^ 1) for j in range(dp_count)]
    )
    held = pair[:, 0] * to_column + arrived.astype(jnp.float32)
    bits = list(range(1, dp_count.bit_length() - 1))
    half = tokens_all // 2
    first = reduce_bits(held[:, :, :half], bits, True)
    second = reduce_bits(held[:, :, half:], bits[::-1], False)
    held = jnp.concatenate([first, second], axis=2)

    stage = 1
    while stage < vocab_count:
        pairs = [(j, j ^ stage) for j in range(vocab_count)]
        teacher_stats = merge(teacher_stats, lax.ppermute(teacher_stats, "vocab", pairs))[0]
        student_stats = merge(student_stats, lax.ppermute(student_stats, "vocab", pairs))[0]
        stage *= 2
    teacher_peak, target_total = teacher_stats[0], teacher_stats[1]
    student_peak, student_total = student_stats[0], student_stats[1]
    mapped = jnp.transpose(
        held[0] * jnp.exp(column_peak - teacher_peak)[None, :, None], (1, 0, 2)
    ).reshape(tokens_all, student_cols)

    target_probs = mapped / target_total[:, None]
    student_probs = jnp.exp(student_logits - student_peak[:, None]) / student_total[:, None]
    columns = device_flat * student_cols + jnp.arange(student_cols, dtype=jnp.int32)
    target_hits = (all_targets[:, None] == columns[None, :]).astype(jnp.float32)
    logit_grad = (
        loss_scale
        * (student_probs - (1.0 - hard_weight) * target_probs - hard_weight * target_hits)
    ).astype(jnp.bfloat16)
    partial = lax.dot_general(
        logit_grad, student_head, (((1,), (1,)), ((), ())), preferred_element_type=jnp.float32
    ).astype(jnp.bfloat16)
    shard_count = dp_count * vocab_count
    partial = partial.reshape(shard_count, tokens_all // shard_count, partial.shape[1])
    received = lax.all_to_all(partial, ("dp", "vocab"), split_axis=0, concat_axis=0, tiled=True)
    gradient = jnp.sum(received.astype(jnp.float32), axis=0)
    return gradient.astype(jnp.bfloat16)


def solution(mesh):
    placed = (
        P(("groups", "dp"), None),
        P(None, ("dp", "vocab")),
        P(("dp", "vocab"), None),
        P(("dp", "vocab"), None),
        P(("dp", "vocab"), None, None, None),
        P(("groups", "dp"), None),
        P(None, ("dp", "vocab")),
        P(("groups", "dp")),
    )
    return jax.shard_map(
        on_device,
        mesh=mesh,
        in_specs=placed,
        out_specs=P(("groups", "dp", "vocab"), None),
        check_vma=False,
    )
```

```python
import jax
import jax.numpy as jnp
from jax import lax
from jax.sharding import PartitionSpec as P

hard_weight = 0.25
loss_scale = 64.0


def _code(values):
    return values.astype(jnp.float32).astype(jnp.bfloat16)


def _decode(values):
    return jnp.round(values.astype(jnp.float32)).astype(jnp.int32)


def on_device(
    teacher_hidden,
    teacher_head,
    map_dest,
    map_slot,
    map_weight,
    student_hidden,
    student_head,
    targets,
):
    dp_count = lax.axis_size("dp")
    vocab_count = lax.axis_size("vocab")
    my_dp = lax.axis_index("dp")
    my_vocab = lax.axis_index("vocab")
    block_size = map_weight.shape[2]
    teacher_blocks = map_dest.shape[0]
    fan_count = map_dest.shape[1]
    student_cols = student_head.shape[1]
    student_blocks = student_cols // block_size
    device_flat = my_dp * vocab_count + my_vocab
    item_count = teacher_blocks * fan_count
    local_tokens = teacher_hidden.shape[0]
    teacher_width = teacher_hidden.shape[1]
    student_width = student_hidden.shape[1]

    coded = jnp.concatenate([_code(targets // 256), _code(targets % 256)])
    extra_width = -(-coded.shape[0] // local_tokens)
    extra_width = -(-extra_width // 128) * 128
    coded = jnp.pad(coded, (0, extra_width * local_tokens - coded.shape[0]))
    packed = jnp.concatenate(
        [teacher_hidden, coded.reshape(local_tokens, extra_width)], axis=1
    )
    gathered = lax.all_gather(packed, "dp", axis=0, tiled=True)
    student_all = lax.all_to_all(
        jnp.broadcast_to(student_hidden[None], (dp_count,) + student_hidden.shape),
        "dp", split_axis=0, concat_axis=0, tiled=True,
    ).reshape(dp_count * local_tokens, student_width)
    tokens_all = gathered.shape[0]
    teacher_all = gathered[:, :teacher_width]
    extra_all = gathered[:, teacher_width:].reshape(dp_count, local_tokens * extra_width)
    t_hi = _decode(extra_all[:, :local_tokens])
    t_lo = _decode(extra_all[:, local_tokens : 2 * local_tokens])
    all_targets = (t_hi * 256 + t_lo).reshape(tokens_all)

    teacher_logits = jnp.dot(teacher_all, teacher_head, preferred_element_type=jnp.float32)
    teacher_local_peak = jnp.max(teacher_logits, axis=1)
    teacher_weights = jnp.exp(teacher_logits - teacher_local_peak[:, None]).astype(jnp.bfloat16)
    prob_blocks = teacher_weights.reshape(tokens_all, teacher_blocks, block_size)
    mapped_terms = jnp.einsum(
        "gkc,krcd->krgd", prob_blocks, map_weight, preferred_element_type=jnp.float32
    ).astype(jnp.bfloat16)
    mapped_mass = jnp.sum(mapped_terms.astype(jnp.float32), axis=(0, 1, 3))

    relative = jnp.bitwise_xor(map_dest.reshape(item_count), my_dp)
    row = relative * student_blocks + map_slot.reshape(item_count)
    placement = (
        jnp.arange(dp_count * student_blocks, dtype=jnp.int32)[:, None] == row[None, :]
    ).astype(jnp.bfloat16)
    held = jnp.einsum(
        "xkr,krgd->xgd",
        placement.reshape(dp_count * student_blocks, teacher_blocks, fan_count),
        mapped_terms,
        preferred_element_type=jnp.float32,
    ).reshape(dp_count, student_blocks, tokens_all, block_size)

    student_logits = jnp.dot(student_all, student_head, preferred_element_type=jnp.float32)
    student_local_peak = jnp.max(student_logits, axis=1)
    student_local_total = jnp.sum(jnp.exp(student_logits - student_local_peak[:, None]), axis=1)

    peak, mass = teacher_local_peak, mapped_mass
    s_peak, s_total = student_local_peak, student_local_total

    def merge(stats, other):
        new_peak = jnp.maximum(stats[0], other[0])
        own, far = jnp.exp(stats[0] - new_peak), jnp.exp(other[0] - new_peak)
        return jnp.stack([new_peak, stats[1] * own + other[1] * far]), own, far

    teacher_stats = jnp.stack([peak, mass])
    student_stats = jnp.stack([s_peak, s_total])
    stage = 1
    while stage < dp_count:
        pairs = [(j, j ^ stage) for j in range(dp_count)]
        teacher_stats = merge(teacher_stats, lax.ppermute(teacher_stats, "dp", pairs))[0]
        student_stats = merge(student_stats, lax.ppermute(student_stats, "dp", pairs))[0]
        stage *= 2
    column_peak = teacher_stats[0]
    to_column = jnp.exp(teacher_local_peak - column_peak)[None, None, :, None]

    def reduce_bits(part, bits, low_first):
        for bit in bits:
            pairs = [(j, j ^ (1 << bit)) for j in range(dp_count)]
            count = part.shape[0] // 2
            if low_first:
                split = part.reshape((count, 2) + part.shape[1:])
                keep, send = split[:, 0], split[:, 1]
            else:
                split = part.reshape((2, count) + part.shape[1:])
                keep, send = split[0], split[1]
            part = keep + lax.ppermute(send.astype(jnp.bfloat16), "dp", pairs).astype(
                jnp.float32
            )
        return part

    pair = held.reshape((held.shape[0] // 2, 2) + held.shape[1:])
    arrived = lax.ppermute(
        (pair[:, 1] * to_column).astype(jnp.bfloat16), "dp", [(j, j ^ 1) for j in range(dp_count)]
    )
    held = pair[:, 0] * to_column + arrived.astype(jnp.float32)
    bits = list(range(1, dp_count.bit_length() - 1))
    half = tokens_all // 2
    first = reduce_bits(held[:, :, :half], bits, True)
    second = reduce_bits(held[:, :, half:], bits[::-1], False)
    held = jnp.concatenate([first, second], axis=2)

    stage = 1
    while stage < vocab_count:
        pairs = [(j, j ^ stage) for j in range(vocab_count)]
        teacher_stats = merge(teacher_stats, lax.ppermute(teacher_stats, "vocab", pairs))[0]
        student_stats = merge(student_stats, lax.ppermute(student_stats, "vocab", pairs))[0]
        stage *= 2
    teacher_peak, target_total = teacher_stats[0], teacher_stats[1]
    student_peak, student_total = student_stats[0], student_stats[1]
    mapped = jnp.transpose(
        held[0] * jnp.exp(column_peak - teacher_peak)[None, :, None], (1, 0, 2)
    ).reshape(tokens_all, student_cols)

    target_probs = mapped / target_total[:, None]
    student_probs = jnp.exp(student_logits - student_peak[:, None]) / student_total[:, None]
    columns = device_flat * student_cols + jnp.arange(student_cols, dtype=jnp.int32)
    target_hits = (all_targets[:, None] == columns[None, :]).astype(jnp.float32)
    logit_grad = (
        loss_scale
        * (student_probs - (1.0 - hard_weight) * target_probs - hard_weight * target_hits)
    ).astype(jnp.bfloat16)
    partial = lax.dot_general(
        logit_grad, student_head, (((1,), (1,)), ((), ())), preferred_element_type=jnp.float32
    ).astype(jnp.bfloat16)
    shard_count = dp_count * vocab_count
    partial = partial.reshape(shard_count, tokens_all // shard_count, partial.shape[1])
    received = lax.all_to_all(partial, ("dp", "vocab"), split_axis=0, concat_axis=0, tiled=True)
    gradient = jnp.sum(received.astype(jnp.float32), axis=0)
    return gradient.astype(jnp.bfloat16)


def solution(mesh):
    placed = (
        P(("groups", "dp"), None),
        P(None, ("dp", "vocab")),
        P(("dp", "vocab"), None),
        P(("dp", "vocab"), None),
        P(("dp", "vocab"), None, None, None),
        P(("groups", "dp"), None),
        P(None, ("dp", "vocab")),
        P(("groups", "dp")),
    )
    return jax.shard_map(
        on_device,
        mesh=mesh,
        in_specs=placed,
        out_specs=P(("groups", "dp", "vocab"), None),
        check_vma=False,
    )
```

```python
import jax
import jax.numpy as jnp
from jax import lax
from jax.sharding import PartitionSpec as P

hard_weight = 0.25
loss_scale = 64.0


def _code(values):
    return values.astype(jnp.float32).astype(jnp.bfloat16)


def _decode(values):
    return jnp.round(values.astype(jnp.float32)).astype(jnp.int32)


def on_device(
    teacher_hidden,
    teacher_head,
    map_dest,
    map_slot,
    map_weight,
    student_hidden,
    student_head,
    targets,
):
    dp_count = lax.axis_size("dp")
    vocab_count = lax.axis_size("vocab")
    my_dp = lax.axis_index("dp")
    my_vocab = lax.axis_index("vocab")
    block_size = map_weight.shape[2]
    teacher_blocks = map_dest.shape[0]
    fan_count = map_dest.shape[1]
    student_cols = student_head.shape[1]
    student_blocks = student_cols // block_size
    device_flat = my_dp * vocab_count + my_vocab
    item_count = teacher_blocks * fan_count
    local_tokens = teacher_hidden.shape[0]
    teacher_width = teacher_hidden.shape[1]
    student_width = student_hidden.shape[1]

    coded = jnp.concatenate([_code(targets // 256), _code(targets % 256)])
    extra_width = -(-coded.shape[0] // local_tokens)
    extra_width = -(-extra_width // 128) * 128
    coded = jnp.pad(coded, (0, extra_width * local_tokens - coded.shape[0]))
    packed = jnp.concatenate(
        [teacher_hidden, coded.reshape(local_tokens, extra_width)], axis=1
    )
    gathered = lax.all_gather(packed, "dp", axis=0, tiled=True)
    student_all = lax.all_to_all(
        jnp.broadcast_to(student_hidden[None], (dp_count,) + student_hidden.shape),
        "dp", split_axis=0, concat_axis=0, tiled=True,
    ).reshape(dp_count * local_tokens, student_width)
    tokens_all = gathered.shape[0]
    teacher_all = gathered[:, :teacher_width]
    extra_all = gathered[:, teacher_width:].reshape(dp_count, local_tokens * extra_width)
    t_hi = _decode(extra_all[:, :local_tokens])
    t_lo = _decode(extra_all[:, local_tokens : 2 * local_tokens])
    all_targets = (t_hi * 256 + t_lo).reshape(tokens_all)

    teacher_logits = jnp.dot(teacher_all, teacher_head, preferred_element_type=jnp.float32)
    teacher_local_peak = jnp.max(teacher_logits, axis=1)
    teacher_weights = jnp.exp(teacher_logits - teacher_local_peak[:, None]).astype(jnp.bfloat16)
    prob_blocks = teacher_weights.reshape(tokens_all, teacher_blocks, block_size)
    mapped_terms = jnp.einsum(
        "gkc,krcd->krgd", prob_blocks, map_weight, preferred_element_type=jnp.float32
    ).astype(jnp.bfloat16)
    mapped_mass = jnp.sum(mapped_terms.astype(jnp.float32), axis=(0, 1, 3))

    relative = jnp.bitwise_xor(map_dest.reshape(item_count), my_dp)
    row = relative * student_blocks + map_slot.reshape(item_count)
    placement = (
        jnp.arange(dp_count * student_blocks, dtype=jnp.int32)[:, None] == row[None, :]
    ).astype(jnp.bfloat16)
    held = jnp.dot(
        placement,
        mapped_terms.reshape(item_count, tokens_all * block_size),
        preferred_element_type=jnp.float32,
    ).reshape(dp_count, student_blocks, tokens_all, block_size)

    student_logits = jnp.dot(student_all, student_head, preferred_element_type=jnp.float32)
    student_local_peak = jnp.max(student_logits, axis=1)
    student_local_total = jnp.sum(jnp.exp(student_logits - student_local_peak[:, None]), axis=1)

    peak, mass = teacher_local_peak, mapped_mass
    s_peak, s_total = student_local_peak, student_local_total

    def merge(stats, other):
        new_peak = jnp.maximum(stats[0], other[0])
        own, far = jnp.exp(stats[0] - new_peak), jnp.exp(other[0] - new_peak)
        return jnp.stack([new_peak, stats[1] * own + other[1] * far]), own, far

    teacher_stats = jnp.stack([peak, mass])
    student_stats = jnp.stack([s_peak, s_total])
    stage = 1
    while stage < dp_count:
        pairs = [(j, j ^ stage) for j in range(dp_count)]
        teacher_stats = merge(teacher_stats, lax.ppermute(teacher_stats, "dp", pairs))[0]
        student_stats = merge(student_stats, lax.ppermute(student_stats, "dp", pairs))[0]
        stage *= 2
    column_peak = teacher_stats[0]
    to_column = jnp.exp(teacher_local_peak - column_peak)[None, None, :, None]

    def reduce_bits(part, bits, low_first):
        for bit in bits:
            pairs = [(j, j ^ (1 << bit)) for j in range(dp_count)]
            count = part.shape[0] // 2
            if low_first:
                split = part.reshape((count, 2) + part.shape[1:])
                keep, send = split[:, 0], split[:, 1]
            else:
                split = part.reshape((2, count) + part.shape[1:])
                keep, send = split[0], split[1]
            part = keep + lax.ppermute(send.astype(jnp.bfloat16), "dp", pairs).astype(
                jnp.float32
            )
        return part

    pair = held.reshape((held.shape[0] // 2, 2) + held.shape[1:])
    arrived = lax.ppermute(
        (pair[:, 1] * to_column).astype(jnp.bfloat16), "dp", [(j, j ^ 1) for j in range(dp_count)]
    )
    held = pair[:, 0] * to_column + arrived.astype(jnp.float32)
    bits = list(range(1, dp_count.bit_length() - 1))
    half = tokens_all // 2
    first = reduce_bits(held[:, :, :half], bits, True)
    second = reduce_bits(held[:, :, half:], bits[::-1], False)
    held = jnp.concatenate([first, second], axis=2)

    stage = 1
    while stage < vocab_count:
        pairs = [(j, j ^ stage) for j in range(vocab_count)]
        both = lax.ppermute(jnp.concatenate([teacher_stats, student_stats]), "vocab", pairs)
        teacher_stats = merge(teacher_stats, both[:2])[0]
        student_stats = merge(student_stats, both[2:])[0]
        stage *= 2
    teacher_peak, target_total = teacher_stats[0], teacher_stats[1]
    student_peak, student_total = student_stats[0], student_stats[1]
    mapped = jnp.transpose(
        held[0] * jnp.exp(column_peak - teacher_peak)[None, :, None], (1, 0, 2)
    ).reshape(tokens_all, student_cols)

    target_probs = mapped / target_total[:, None]
    student_probs = jnp.exp(student_logits - student_peak[:, None]) / student_total[:, None]
    columns = device_flat * student_cols + jnp.arange(student_cols, dtype=jnp.int32)
    target_hits = (all_targets[:, None] == columns[None, :]).astype(jnp.float32)
    logit_grad = (
        loss_scale
        * (student_probs - (1.0 - hard_weight) * target_probs - hard_weight * target_hits)
    ).astype(jnp.bfloat16)
    partial = lax.dot_general(
        logit_grad, student_head, (((1,), (1,)), ((), ())), preferred_element_type=jnp.float32
    ).astype(jnp.bfloat16)
    shard_count = dp_count * vocab_count
    partial = partial.reshape(shard_count, tokens_all // shard_count, partial.shape[1])
    received = lax.all_to_all(partial, ("dp", "vocab"), split_axis=0, concat_axis=0, tiled=True)
    gradient = jnp.sum(received.astype(jnp.float32), axis=0)
    return gradient.astype(jnp.bfloat16)


def solution(mesh):
    placed = (
        P(("groups", "dp"), None),
        P(None, ("dp", "vocab")),
        P(("dp", "vocab"), None),
        P(("dp", "vocab"), None),
        P(("dp", "vocab"), None, None, None),
        P(("groups", "dp"), None),
        P(None, ("dp", "vocab")),
        P(("groups", "dp")),
    )
    return jax.shard_map(
        on_device,
        mesh=mesh,
        in_specs=placed,
        out_specs=P(("groups", "dp", "vocab"), None),
        check_vma=False,
    )
```

```python
import jax
import jax.numpy as jnp
from jax import lax
from jax.sharding import PartitionSpec as P

hard_weight = 0.25
loss_scale = 64.0


def _code(values):
    return values.astype(jnp.float32).astype(jnp.bfloat16)


def _decode(values):
    return jnp.round(values.astype(jnp.float32)).astype(jnp.int32)


def on_device(
    teacher_hidden,
    teacher_head,
    map_dest,
    map_slot,
    map_weight,
    student_hidden,
    student_head,
    targets,
):
    dp_count = lax.axis_size("dp")
    vocab_count = lax.axis_size("vocab")
    my_dp = lax.axis_index("dp")
    my_vocab = lax.axis_index("vocab")
    block_size = map_weight.shape[2]
    teacher_blocks = map_dest.shape[0]
    fan_count = map_dest.shape[1]
    student_cols = student_head.shape[1]
    student_blocks = student_cols // block_size
    device_flat = my_dp * vocab_count + my_vocab
    item_count = teacher_blocks * fan_count
    local_tokens = teacher_hidden.shape[0]
    teacher_width = teacher_hidden.shape[1]
    student_width = student_hidden.shape[1]

    coded = jnp.concatenate([_code(targets // 256), _code(targets % 256)])
    extra_width = -(-coded.shape[0] // local_tokens)
    extra_width = -(-extra_width // 128) * 128
    coded = jnp.pad(coded, (0, extra_width * local_tokens - coded.shape[0]))
    packed = jnp.concatenate(
        [teacher_hidden, coded.reshape(local_tokens, extra_width)], axis=1
    )
    gathered = lax.all_gather(packed, "dp", axis=0, tiled=True)
    student_all = lax.all_to_all(
        jnp.broadcast_to(student_hidden[None], (dp_count,) + student_hidden.shape),
        "dp", split_axis=0, concat_axis=0, tiled=True,
    ).reshape(dp_count * local_tokens, student_width)
    tokens_all = gathered.shape[0]
    teacher_all = gathered[:, :teacher_width]
    extra_all = gathered[:, teacher_width:].reshape(dp_count, local_tokens * extra_width)
    t_hi = _decode(extra_all[:, :local_tokens])
    t_lo = _decode(extra_all[:, local_tokens : 2 * local_tokens])
    all_targets = (t_hi * 256 + t_lo).reshape(tokens_all)

    teacher_logits = jnp.dot(teacher_all, teacher_head, preferred_element_type=jnp.float32)
    teacher_local_peak = jnp.max(teacher_logits, axis=1)
    teacher_weights = jnp.exp(teacher_logits - teacher_local_peak[:, None]).astype(jnp.bfloat16)
    prob_blocks = teacher_weights.reshape(tokens_all, teacher_blocks, block_size)
    mapped_terms = jnp.einsum(
        "gkc,krcd->krgd", prob_blocks, map_weight, preferred_element_type=jnp.float32
    ).astype(jnp.bfloat16)
    mapped_mass = jnp.sum(mapped_terms.astype(jnp.float32), axis=(0, 1, 3))

    relative = jnp.bitwise_xor(map_dest.reshape(item_count), my_dp)
    row = relative * student_blocks + map_slot.reshape(item_count)
    placement = (
        jnp.arange(dp_count * student_blocks, dtype=jnp.int32)[:, None] == row[None, :]
    ).astype(jnp.bfloat16)
    held = jnp.dot(
        placement,
        mapped_terms.reshape(item_count, tokens_all * block_size),
        preferred_element_type=jnp.float32,
    ).reshape(dp_count, student_blocks, tokens_all, block_size)

    student_logits = jnp.dot(student_all, student_head, preferred_element_type=jnp.float32)
    student_local_peak = jnp.max(student_logits, axis=1)
    student_local_total = jnp.sum(jnp.exp(student_logits - student_local_peak[:, None]), axis=1)

    peak, mass = teacher_local_peak, mapped_mass
    s_peak, s_total = student_local_peak, student_local_total

    def merge(stats, other):
        new_peak = jnp.maximum(stats[0], other[0])
        own, far = jnp.exp(stats[0] - new_peak), jnp.exp(other[0] - new_peak)
        return jnp.stack([new_peak, stats[1] * own + other[1] * far]), own, far

    teacher_stats = jnp.stack([peak, mass])
    student_stats = jnp.stack([s_peak, s_total])
    stage = 1
    while stage < dp_count:
        pairs = [(j, j ^ stage) for j in range(dp_count)]
        teacher_stats = merge(teacher_stats, lax.ppermute(teacher_stats, "dp", pairs))[0]
        student_stats = merge(student_stats, lax.ppermute(student_stats, "dp", pairs))[0]
        stage *= 2
    column_peak = teacher_stats[0]
    to_column = jnp.exp(teacher_local_peak - column_peak)[None, None, :, None]

    def reduce_bits(part, bits, low_first):
        for bit in bits:
            pairs = [(j, j ^ (1 << bit)) for j in range(dp_count)]
            count = part.shape[0] // 2
            if low_first:
                split = part.reshape((count, 2) + part.shape[1:])
                keep, send = split[:, 0], split[:, 1]
            else:
                split = part.reshape((2, count) + part.shape[1:])
                keep, send = split[0], split[1]
            part = keep + lax.ppermute(send.astype(jnp.bfloat16), "dp", pairs).astype(
                jnp.float32
            )
        return part

    pair = held.reshape((held.shape[0] // 2, 2) + held.shape[1:])
    arrived = lax.ppermute(
        (pair[:, 1] * to_column).astype(jnp.bfloat16), "dp", [(j, j ^ 1) for j in range(dp_count)]
    )
    held = pair[:, 0] * to_column + arrived.astype(jnp.float32)
    held, teacher_stats = lax.optimization_barrier((held, teacher_stats))
    bits = list(range(1, dp_count.bit_length() - 1))
    half = tokens_all // 2
    first = reduce_bits(held[:, :, :half], bits, True)
    second = reduce_bits(held[:, :, half:], bits[::-1], False)
    held = jnp.concatenate([first, second], axis=2)

    stage = 1
    while stage < vocab_count:
        pairs = [(j, j ^ stage) for j in range(vocab_count)]
        teacher_stats = merge(teacher_stats, lax.ppermute(teacher_stats, "vocab", pairs))[0]
        student_stats = merge(student_stats, lax.ppermute(student_stats, "vocab", pairs))[0]
        stage *= 2
    teacher_peak, target_total = teacher_stats[0], teacher_stats[1]
    student_peak, student_total = student_stats[0], student_stats[1]
    mapped = jnp.transpose(
        held[0] * jnp.exp(column_peak - teacher_peak)[None, :, None], (1, 0, 2)
    ).reshape(tokens_all, student_cols)

    target_probs = mapped / target_total[:, None]
    student_probs = jnp.exp(student_logits - student_peak[:, None]) / student_total[:, None]
    columns = device_flat * student_cols + jnp.arange(student_cols, dtype=jnp.int32)
    target_hits = (all_targets[:, None] == columns[None, :]).astype(jnp.float32)
    logit_grad = (
        loss_scale
        * (student_probs - (1.0 - hard_weight) * target_probs - hard_weight * target_hits)
    ).astype(jnp.bfloat16)
    partial = lax.dot_general(
        logit_grad, student_head, (((1,), (1,)), ((), ())), preferred_element_type=jnp.float32
    ).astype(jnp.bfloat16)
    shard_count = dp_count * vocab_count
    partial = partial.reshape(shard_count, tokens_all // shard_count, partial.shape[1])
    received = lax.all_to_all(partial, ("dp", "vocab"), split_axis=0, concat_axis=0, tiled=True)
    gradient = jnp.sum(received.astype(jnp.float32), axis=0)
    return gradient.astype(jnp.bfloat16)


def solution(mesh):
    placed = (
        P(("groups", "dp"), None),
        P(None, ("dp", "vocab")),
        P(("dp", "vocab"), None),
        P(("dp", "vocab"), None),
        P(("dp", "vocab"), None, None, None),
        P(("groups", "dp"), None),
        P(None, ("dp", "vocab")),
        P(("groups", "dp")),
    )
    return jax.shard_map(
        on_device,
        mesh=mesh,
        in_specs=placed,
        out_specs=P(("groups", "dp", "vocab"), None),
        check_vma=False,
    )
```

```python
import jax
import jax.numpy as jnp
from jax import lax
from jax.sharding import PartitionSpec as P

hard_weight = 0.25
loss_scale = 64.0


def _code(values):
    return values.astype(jnp.float32).astype(jnp.bfloat16)


def _decode(values):
    return jnp.round(values.astype(jnp.float32)).astype(jnp.int32)


def on_device(
    teacher_hidden,
    teacher_head,
    map_dest,
    map_slot,
    map_weight,
    student_hidden,
    student_head,
    targets,
):
    dp_count = lax.axis_size("dp")
    vocab_count = lax.axis_size("vocab")
    my_dp = lax.axis_index("dp")
    my_vocab = lax.axis_index("vocab")
    block_size = map_weight.shape[2]
    teacher_blocks = map_dest.shape[0]
    fan_count = map_dest.shape[1]
    student_cols = student_head.shape[1]
    student_blocks = student_cols // block_size
    device_flat = my_dp * vocab_count + my_vocab
    item_count = teacher_blocks * fan_count
    local_tokens = teacher_hidden.shape[0]
    teacher_width = teacher_hidden.shape[1]
    student_width = student_hidden.shape[1]

    coded = jnp.concatenate([_code(targets // 256), _code(targets % 256)])
    extra_width = -(-coded.shape[0] // local_tokens)
    extra_width = -(-extra_width // 128) * 128
    coded = jnp.pad(coded, (0, extra_width * local_tokens - coded.shape[0]))
    packed = jnp.concatenate(
        [teacher_hidden, coded.reshape(local_tokens, extra_width)], axis=1
    )
    gathered = lax.all_gather(packed, "dp", axis=0, tiled=True)
    student_all = lax.all_gather(
        jnp.pad(student_hidden, ((0, 0), (0, teacher_width + extra_width))),
        "dp", axis=0, tiled=True,
    )[:, :student_width]
    tokens_all = gathered.shape[0]
    teacher_all = gathered[:, :teacher_width]
    extra_all = gathered[:, teacher_width:].reshape(dp_count, local_tokens * extra_width)
    t_hi = _decode(extra_all[:, :local_tokens])
    t_lo = _decode(extra_all[:, local_tokens : 2 * local_tokens])
    all_targets = (t_hi * 256 + t_lo).reshape(tokens_all)

    teacher_logits = jnp.dot(teacher_all, teacher_head, preferred_element_type=jnp.float32)
    teacher_local_peak = jnp.max(teacher_logits, axis=1)
    teacher_weights = jnp.exp(teacher_logits - teacher_local_peak[:, None]).astype(jnp.bfloat16)
    prob_blocks = teacher_weights.reshape(tokens_all, teacher_blocks, block_size)
    mapped_terms = jnp.einsum(
        "gkc,krcd->krgd", prob_blocks, map_weight, preferred_element_type=jnp.float32
    ).astype(jnp.bfloat16)
    mapped_mass = jnp.sum(mapped_terms.astype(jnp.float32), axis=(0, 1, 3))

    relative = jnp.bitwise_xor(map_dest.reshape(item_count), my_dp)
    row = relative * student_blocks + map_slot.reshape(item_count)
    placement = (
        jnp.arange(dp_count * student_blocks, dtype=jnp.int32)[:, None] == row[None, :]
    ).astype(jnp.bfloat16)
    held = jnp.dot(
        placement,
        mapped_terms.reshape(item_count, tokens_all * block_size),
        preferred_element_type=jnp.float32,
    ).reshape(dp_count, student_blocks, tokens_all, block_size)

    student_logits = jnp.dot(student_all, student_head, preferred_element_type=jnp.float32)
    student_local_peak = jnp.max(student_logits, axis=1)
    student_local_total = jnp.sum(jnp.exp(student_logits - student_local_peak[:, None]), axis=1)

    peak, mass = teacher_local_peak, mapped_mass
    s_peak, s_total = student_local_peak, student_local_total

    def merge(stats, other):
        new_peak = jnp.maximum(stats[0], other[0])
        own, far = jnp.exp(stats[0] - new_peak), jnp.exp(other[0] - new_peak)
        return jnp.stack([new_peak, stats[1] * own + other[1] * far]), own, far

    teacher_stats = jnp.stack([peak, mass])
    student_stats = jnp.stack([s_peak, s_total])
    stage = 1
    while stage < dp_count:
        pairs = [(j, j ^ stage) for j in range(dp_count)]
        teacher_stats = merge(teacher_stats, lax.ppermute(teacher_stats, "dp", pairs))[0]
        student_stats = merge(student_stats, lax.ppermute(student_stats, "dp", pairs))[0]
        stage *= 2
    column_peak = teacher_stats[0]
    to_column = jnp.exp(teacher_local_peak - column_peak)[None, None, :, None]

    def reduce_bits(part, bits, low_first):
        for bit in bits:
            pairs = [(j, j ^ (1 << bit)) for j in range(dp_count)]
            count = part.shape[0] // 2
            if low_first:
                split = part.reshape((count, 2) + part.shape[1:])
                keep, send = split[:, 0], split[:, 1]
            else:
                split = part.reshape((2, count) + part.shape[1:])
                keep, send = split[0], split[1]
            part = keep + lax.ppermute(send.astype(jnp.bfloat16), "dp", pairs).astype(
                jnp.float32
            )
        return part

    pair = held.reshape((held.shape[0] // 2, 2) + held.shape[1:])
    arrived = lax.ppermute(
        (pair[:, 1] * to_column).astype(jnp.bfloat16), "dp", [(j, j ^ 1) for j in range(dp_count)]
    )
    held = pair[:, 0] * to_column + arrived.astype(jnp.float32)
    bits = list(range(1, dp_count.bit_length() - 1))
    half = tokens_all // 2
    first = reduce_bits(held[:, :, :half], bits, True)
    second = reduce_bits(held[:, :, half:], bits[::-1], False)
    held = jnp.concatenate([first, second], axis=2)

    stage = 1
    while stage < vocab_count:
        pairs = [(j, j ^ stage) for j in range(vocab_count)]
        teacher_stats = merge(teacher_stats, lax.ppermute(teacher_stats, "vocab", pairs))[0]
        student_stats = merge(student_stats, lax.ppermute(student_stats, "vocab", pairs))[0]
        stage *= 2
    teacher_peak, target_total = teacher_stats[0], teacher_stats[1]
    student_peak, student_total = student_stats[0], student_stats[1]
    mapped = jnp.transpose(
        held[0] * jnp.exp(column_peak - teacher_peak)[None, :, None], (1, 0, 2)
    ).reshape(tokens_all, student_cols)

    target_probs = mapped / target_total[:, None]
    student_probs = jnp.exp(student_logits - student_peak[:, None]) / student_total[:, None]
    columns = device_flat * student_cols + jnp.arange(student_cols, dtype=jnp.int32)
    target_hits = (all_targets[:, None] == columns[None, :]).astype(jnp.float32)
    logit_grad = (
        loss_scale
        * (student_probs - (1.0 - hard_weight) * target_probs - hard_weight * target_hits)
    ).astype(jnp.bfloat16)
    partial = lax.dot_general(
        logit_grad, student_head, (((1,), (1,)), ((), ())), preferred_element_type=jnp.float32
    ).astype(jnp.bfloat16)
    shard_count = dp_count * vocab_count
    partial = partial.reshape(shard_count, tokens_all // shard_count, partial.shape[1])
    received = lax.all_to_all(partial, ("dp", "vocab"), split_axis=0, concat_axis=0, tiled=True)
    gradient = jnp.sum(received.astype(jnp.float32), axis=0)
    return gradient.astype(jnp.bfloat16)


def solution(mesh):
    placed = (
        P(("groups", "dp"), None),
        P(None, ("dp", "vocab")),
        P(("dp", "vocab"), None),
        P(("dp", "vocab"), None),
        P(("dp", "vocab"), None, None, None),
        P(("groups", "dp"), None),
        P(None, ("dp", "vocab")),
        P(("groups", "dp")),
    )
    return jax.shard_map(
        on_device,
        mesh=mesh,
        in_specs=placed,
        out_specs=P(("groups", "dp", "vocab"), None),
        check_vma=False,
    )
```
